512 devices in a mesh: frames: 64 (over y, z), atoms: 8 (over x, core).
Axes of the slice: x: 4, y: 8, z: 8, core: 2. Of those that a mesh axis runs over, the one named last changes fastest.
Arguments:
- displacements: float32 [1024, 3, 16384], P('frames', None, 'atoms'), may hold values from -2 to 2
Outputs:
- msd: float32 [16384, 1024], P(('atoms', 'frames'))
The draws below stay inside these ranges and needn't reach their ends.
All inputs are finite; a program needn't handle non-finite values.
Results may differ from the reference program's by a relative error of at most 0.0003.
Values sent between devices are 32-bit elements; how exact they have to be, the bound alone decides.
No kernel may reach another device: no remote copies, remote signals or barrier semaphores. Data moves between devices by JAX's collectives and lax.ppermute only.
A program may use at most 64 MiB of HBM per device.

```python
import math
import jax
import jax.numpy as jnp
from jax import lax

LENGTH = 1024
ATOMS = 16384


def draw_displacements(key, part):
    key_noise = jax.random.fold_in(key, 0)
    key_weight = jax.random.fold_in(key, 2)
    key_drift = jax.random.fold_in(key, 3)
    noise = jnp.clip(jax.random.normal(key_noise, (LENGTH, 3, ATOMS), jnp.float32), -5.0, 5.0)
    scale_atom = jnp.ones((1, 1, ATOMS), jnp.float32)
    drift_size = 0.09
    index = jnp.arange(ATOMS).astype(jnp.float32)
    weight_atom = 2.0 * (index + 0.5) / ATOMS * jax.random.uniform(key_weight, (ATOMS,), jnp.float32, 0.5, 1.5)
    drift = drift_size * jnp.clip(jax.random.normal(key_drift, (LENGTH, 3, 1), jnp.float32), -4.0, 4.0)
    values = 0.03 * scale_atom * noise + drift * weight_atom[None, None, :]
    return jnp.clip(values, -2.0, 2.0).astype(jnp.float32)


def setup_inputs(seed: int = 0) -> dict:
    keys = jax.random.split(jax.random.key(seed), 2)
    displacements = draw_displacements(jax.random.fold_in(keys[1], 71), 0)
    return dict(displacements=displacements)


def reference(displacements):
    drift = jnp.sum(displacements, axis=2) / ATOMS
    positions = jnp.cumsum(displacements - drift[:, :, None], axis=0)
    squares = jnp.sum(positions * positions, axis=1)
    zero_row = jnp.zeros((1, ATOMS), squares.dtype)
    running = jnp.concatenate([zero_row, jnp.cumsum(squares, axis=0)], axis=0)
    head = running[LENGTH][None, :] - running[:LENGTH]
    tail = jnp.flip(running[1:], 0)
    width = math.gcd(ATOMS, 512)
    series = jnp.transpose(positions, (2, 1, 0)).reshape(ATOMS // width, width, 3, LENGTH)

    def correlate(block):
        spectrum = jnp.fft.rfft(block, n=2 * LENGTH, axis=-1)
        power = jnp.sum(jnp.real(spectrum) ** 2 + jnp.imag(spectrum) ** 2, axis=1)
        return jnp.fft.irfft(power, n=2 * LENGTH, axis=-1)[:, :LENGTH]

    corr = lax.map(correlate, series).reshape(ATOMS, LENGTH).astype(positions.dtype)
    counts = (LENGTH - jnp.arange(LENGTH)).astype(positions.dtype)
    return (jnp.transpose(head + tail) - 2.0 * corr) / counts[None, :]
```

```python
import numpy as np

import jax
import jax.numpy as jnp
from jax import lax
from jax.sharding import PartitionSpec as P


def angle_tables(length, split):
    frame = np.arange(length, dtype=np.int64)
    low = np.arange(split, dtype=np.int64)
    high = np.arange(length // split, dtype=np.int64) * split
    coarse = (high[:, None] * frame[None, :]) % (2 * length) * (np.pi / length)
    fine = (low[:, None] * frame[None, :]) % (2 * length) * (np.pi / length)
    return [
        jnp.asarray(t.astype(np.float32))
        for t in (np.cos(coarse), np.sin(coarse), np.cos(fine), np.sin(fine))
    ]


def spectral_tables(length):
    cos_hi, sin_hi, cos_lo, sin_lo = angle_tables(length, 32)
    cosine = (cos_hi[:, None, :] * cos_lo[None, :, :] - sin_hi[:, None, :] * sin_lo[None, :, :])
    sine = (sin_hi[:, None, :] * cos_lo[None, :, :] + cos_hi[:, None, :] * sin_lo[None, :, :])
    cosine = cosine.reshape(length, length)
    sine = sine.reshape(length, length)
    frame = jnp.arange(length, dtype=jnp.int32)
    parity = jnp.where(frame % 2 == 0, 1.0, -1.0).astype(jnp.float32)
    sine = jnp.where((frame == 0)[:, None], parity[None, :], sine)
    return cosine, sine, parity


def lag_table(series, count):
    length = series.shape[0]
    frame = jnp.arange(length, dtype=jnp.int32)
    lower = (frame[None, :] <= frame[:, None]).astype(jnp.float32)
    positions = jnp.dot(lower, series, precision=lax.Precision.HIGHEST)
    squares = jnp.sum((positions * positions).reshape(length, 3, count), axis=1)
    cosine, sine, parity = spectral_tables(length)
    both = jnp.concatenate([cosine, sine], axis=0)
    spectrum = jnp.dot(both, positions, precision=lax.Precision.HIGHEST)
    real_part = spectrum[:length].reshape(length, 3, count)
    imag_part = spectrum[length:].reshape(length, 3, count)
    imag_zeroed = jnp.where((frame == 0)[:, None, None], 0.0, imag_part)
    power = jnp.sum(real_part * real_part + imag_zeroed * imag_zeroed, axis=1)
    power_top = jnp.sum(imag_part[0] * imag_part[0], axis=0)
    window = (
        (frame[None, :] >= frame[:, None]).astype(jnp.float32)
        + (frame[None, :] <= (length - 1 - frame)[:, None]).astype(jnp.float32)
    )
    weight = jnp.where(frame == 0, 1.0, 2.0).astype(jnp.float32) * (2.0 / (2 * length))
    mixing = jnp.concatenate([window, -cosine * weight[None, :]], axis=1)
    stacked = jnp.concatenate([squares, power], axis=0)
    numer = jnp.dot(mixing, stacked, precision=lax.Precision.HIGHEST)
    numer = numer - power_top[None, :] * parity[:, None] * (2.0 / (2 * length))
    counts = (length - frame).astype(jnp.float32)
    return jnp.transpose(numer / counts[:, None])


def per_device(displacements):
    local_frames, _, atom_count = displacements.shape
    groups = lax.axis_size("frames")
    atom_total = atom_count * lax.axis_size("atoms")
    summed = lax.psum(jnp.sum(displacements, axis=2), "atoms")
    centred = displacements - (summed / atom_total)[:, :, None]
    blocks = centred.reshape(local_frames, 3, groups, atom_count // groups)
    moved = lax.all_to_all(blocks, "frames", split_axis=2, concat_axis=0, tiled=True)
    count = atom_count // groups
    series = moved.reshape(local_frames * groups, 3 * count)
    return lag_table(series, count)


def solution(mesh):
    placed = (P("frames", None, "atoms"),)
    return jax.shard_map(
        per_device,
        mesh=mesh,
        in_specs=placed,
        out_specs=P(("atoms", "frames"), None),
        check_vma=False,
    )
```

```python
import numpy as np

import jax
import jax.numpy as jnp
from jax import lax
from jax.sharding import PartitionSpec as P


def angle_tables(length, split):
    frame = np.arange(length, dtype=np.int64)
    low = np.arange(split, dtype=np.int64)
    high = np.arange(length // split, dtype=np.int64) * split
    coarse = (high[:, None] * frame[None, :]) % (2 * length) * (np.pi / length)
    fine = (low[:, None] * frame[None, :]) % (2 * length) * (np.pi / length)
    return [
        jnp.asarray(t.astype(np.float32))
        for t in (np.cos(coarse), np.sin(coarse), np.cos(fine), np.sin(fine))
    ]


def spectral_tables(length, rows):
    split = 32
    cos_hi, sin_hi, cos_lo, sin_lo = angle_tables(length, split)
    blocks = -(-rows // split)
    cos_hi, sin_hi = cos_hi[:blocks], sin_hi[:blocks]
    cosine = cos_hi[:, None, :] * cos_lo[None, :, :] - sin_hi[:, None, :] * sin_lo[None, :, :]
    sine = sin_hi[:, None, :] * cos_lo[None, :, :] + cos_hi[:, None, :] * sin_lo[None, :, :]
    cosine = cosine.reshape(blocks * split, length)[:rows]
    sine = sine.reshape(blocks * split, length)[:rows]
    return cosine, sine


def split_three(values):
    first = lax.reduce_precision(values, exponent_bits=8, mantissa_bits=7)
    rest = values - first
    second = lax.reduce_precision(rest, exponent_bits=8, mantissa_bits=7)
    third = rest - second
    return jnp.concatenate([first, second, third], axis=1).astype(jnp.bfloat16)


def exact_product(matrix, values):
    width = values.shape[1]
    out = jnp.dot(
        matrix.astype(jnp.bfloat16), split_three(values), preferred_element_type=jnp.float32
    )
    return out[:, :width] + out[:, width : 2 * width] + out[:, 2 * width :]


def lag_table(series, count):
    length = series.shape[0]
    half = length // 2
    width = 3 * count
    frame = jnp.arange(length, dtype=jnp.int32)
    lower = (frame[None, :] <= frame[:, None]).astype(jnp.float32)
    positions = exact_product(lower, series)
    squares = jnp.sum((positions * positions).reshape(length, 3, count), axis=1)
    cosine, sine = spectral_tables(length, half + 1)
    parity = jnp.where(frame % 2 == 0, 1.0, -1.0).astype(jnp.float32)
    both = jnp.concatenate([cosine, sine[1:]], axis=0)
    signed = jnp.concatenate([positions, positions * parity[:, None]], axis=1)
    spectrum = jnp.dot(both, signed, precision=lax.Precision.HIGHEST)
    real_part = spectrum[: half + 1]
    imag_part = jnp.concatenate([jnp.zeros((1, 2 * width), jnp.float32), spectrum[half + 1 :]], axis=0)
    power = jnp.sum((real_part * real_part + imag_part * imag_part).reshape(half + 1, 2, 3, count), axis=2)
    low_q = jnp.arange(half, dtype=jnp.int32)
    weight = jnp.where(low_q == 0, 1.0, 2.0).astype(jnp.float32) / (2 * length)
    coef = power[:half] * weight[:, None, None]
    coef = coef.at[:, 1].set(jnp.where((low_q == 0)[:, None], power[0, 1][None, :] / (2 * length), coef[:, 1]))
    sign_q = jnp.where(low_q % 2 == 0, 1.0, -1.0).astype(jnp.float32)
    coef = coef.reshape(half, 2 * count)
    coef = jnp.concatenate([coef, coef * sign_q[:, None]], axis=1)
    middle = power[half, 0] * (2.0 / (2 * length))
    table = cosine[:, :half]
    folded = jnp.dot(table, coef, precision=lax.Precision.HIGHEST)
    lag = jnp.arange(half + 1, dtype=jnp.int32)
    sign_m = jnp.where(lag % 2 == 0, 1.0, -1.0).astype(jnp.float32)[:, None]
    quarter = jnp.where(lag % 4 == 0, 1.0, jnp.where(lag % 4 == 2, -1.0, 0.0)).astype(jnp.float32)[:, None]
    near = folded[:, :count] + sign_m * folded[:, count : 2 * count] + middle[None, :] * quarter
    far = folded[:, 2 * count : 3 * count] + sign_m * folded[:, 3 * count :] + middle[None, :] * quarter
    corr = jnp.concatenate([near, jnp.flip(far[1:half], axis=0)], axis=0)
    window = (
        (frame[None, :] >= frame[:, None]).astype(jnp.float32)
        + (frame[None, :] <= (length - 1 - frame)[:, None]).astype(jnp.float32)
    )
    numer = exact_product(window, squares) - 2.0 * corr
    counts = (length - frame).astype(jnp.float32)
    return jnp.transpose(numer / counts[:, None])


def per_device(displacements):
    local_frames, _, atom_count = displacements.shape
    groups = lax.axis_size("frames")
    atom_total = atom_count * lax.axis_size("atoms")
    summed = lax.psum(jnp.sum(displacements, axis=2), "atoms")
    centred = displacements - (summed / atom_total)[:, :, None]
    blocks = centred.reshape(local_frames, 3, groups, atom_count // groups)
    moved = lax.all_to_all(blocks, "frames", split_axis=2, concat_axis=0, tiled=True)
    count = atom_count // groups
    series = moved.reshape(local_frames * groups, 3 * count)
    return lag_table(series, count)


def solution(mesh):
    placed = (P("frames", None, "atoms"),)
    return jax.shard_map(
        per_device,
        mesh=mesh,
        in_specs=placed,
        out_specs=P(("atoms", "frames"), None),
        check_vma=False,
    )
```

```python
import numpy as np

import jax
import jax.numpy as jnp
from jax import lax
from jax.sharding import PartitionSpec as P


def angle_tables(length, split):
    frame = np.arange(length, dtype=np.int64)
    low = np.arange(split, dtype=np.int64)
    high = np.arange(length // split, dtype=np.int64) * split
    coarse = (high[:, None] * frame[None, :]) % (2 * length) * (np.pi / length)
    fine = (low[:, None] * frame[None, :]) % (2 * length) * (np.pi / length)
    return [
        jnp.asarray(t.astype(np.float32))
        for t in (np.cos(coarse), np.sin(coarse), np.cos(fine), np.sin(fine))
    ]


def spectral_tables(length, rows):
    split = 32
    cos_hi, sin_hi, cos_lo, sin_lo = angle_tables(length, split)
    blocks = -(-rows // split)
    cos_hi, sin_hi = cos_hi[:blocks], sin_hi[:blocks]
    cosine = cos_hi[:, None, :] * cos_lo[None, :, :] - sin_hi[:, None, :] * sin_lo[None, :, :]
    sine = sin_hi[:, None, :] * cos_lo[None, :, :] + cos_hi[:, None, :] * sin_lo[None, :, :]
    cosine = cosine.reshape(blocks * split, length)[:rows]
    sine = sine.reshape(blocks * split, length)[:rows]
    return cosine, sine


def split_three(values):
    first = lax.reduce_precision(values, exponent_bits=8, mantissa_bits=7)
    rest = values - first
    second = lax.reduce_precision(rest, exponent_bits=8, mantissa_bits=7)
    third = rest - second
    return jnp.concatenate([first, second, third], axis=1).astype(jnp.bfloat16)


def exact_product(matrix, values):
    width = values.shape[1]
    out = jnp.dot(
        matrix.astype(jnp.bfloat16), split_three(values), preferred_element_type=jnp.float32
    )
    return out[:, :width] + out[:, width : 2 * width] + out[:, 2 * width :]


def lag_table(series, count):
    length = series.shape[0]
    half = length // 2
    width = 3 * count
    frame = jnp.arange(length, dtype=jnp.int32)
    lower = (frame[None, :] <= frame[:, None]).astype(jnp.float32)
    positions = exact_product(lower, series)
    squares = jnp.sum((positions * positions).reshape(length, 3, count), axis=1)
    cosine, sine = spectral_tables(length, half + 1)
    parity = jnp.where(frame % 2 == 0, 1.0, -1.0).astype(jnp.float32)
    both = jnp.concatenate([cosine, sine[1:]], axis=0)
    signed = jnp.concatenate([positions, positions * parity[:, None]], axis=1)
    spectrum = jnp.dot(both, signed, precision=lax.Precision.HIGHEST)
    real_part = spectrum[: half + 1]
    imag_part = jnp.concatenate([jnp.zeros((1, 2 * width), jnp.float32), spectrum[half + 1 :]], axis=0)
    power = jnp.sum((real_part * real_part + imag_part * imag_part).reshape(half + 1, 2, 3, count), axis=2)
    low_q = jnp.arange(half, dtype=jnp.int32)
    weight = jnp.where(low_q == 0, 1.0, 2.0).astype(jnp.float32) / (2 * length)
    coef = power[:half] * weight[:, None, None]
    coef = coef.at[:, 1].set(jnp.where((low_q == 0)[:, None], power[0, 1][None, :] / (2 * length), coef[:, 1]))
    sign_q = jnp.where(low_q % 2 == 0, 1.0, -1.0).astype(jnp.float32)
    coef = coef.reshape(half, 2 * count)
    coef = jnp.concatenate([coef, coef * sign_q[:, None]], axis=1)
    middle = power[half, 0] * (2.0 / (2 * length))
    table = cosine[:, :half]
    folded = jnp.dot(table, coef, precision=lax.Precision.HIGHEST)
    lag = jnp.arange(half + 1, dtype=jnp.int32)
    sign_m = jnp.where(lag % 2 == 0, 1.0, -1.0).astype(jnp.float32)[:, None]
    quarter = jnp.where(lag % 4 == 0, 1.0, jnp.where(lag % 4 == 2, -1.0, 0.0)).astype(jnp.float32)[:, None]
    near = folded[:, :count] + sign_m * folded[:, count : 2 * count] + middle[None, :] * quarter
    far = folded[:, 2 * count : 3 * count] + sign_m * folded[:, 3 * count :] + middle[None, :] * quarter
    corr = jnp.concatenate([near, jnp.flip(far[1:half], axis=0)], axis=0)
    window = (
        (frame[None, :] >= frame[:, None]).astype(jnp.float32)
        + (frame[None, :] <= (length - 1 - frame)[:, None]).astype(jnp.float32)
    )
    numer = exact_product(window, squares) - 2.0 * corr
    counts = (length - frame).astype(jnp.float32)
    return jnp.transpose(numer / counts[:, None])


def per_device(displacements):
    local_frames, _, atom_count = displacements.shape
    groups = lax.axis_size("frames")
    atom_total = atom_count * lax.axis_size("atoms")
    summed = lax.psum(jnp.sum(displacements, axis=2), "atoms")
    centred = displacements - (summed / atom_total)[:, :, None]
    count = atom_count // groups
    blocks = centred.reshape(local_frames, 3, groups, count)
    outgoing = jnp.transpose(blocks, (2, 0, 1, 3)).reshape(groups, local_frames * 3 * count)
    moved = lax.all_to_all(outgoing, "frames", split_axis=0, concat_axis=0, tiled=True)
    series = moved.reshape(groups * local_frames, 3 * count)
    return lag_table(series, count)


def solution(mesh):
    placed = (P("frames", None, "atoms"),)
    return jax.shard_map(
        per_device,
        mesh=mesh,
        in_specs=placed,
        out_specs=P(("atoms", "frames"), None),
        check_vma=False,
    )
```

```python
import numpy as np

import jax
import jax.numpy as jnp
from jax import lax
from jax.sharding import PartitionSpec as P


def angle_tables(length, split):
    frame = np.arange(length, dtype=np.int64)
    low = np.arange(split, dtype=np.int64)
    high = np.arange(length // split, dtype=np.int64) * split
    coarse = (high[:, None] * frame[None, :]) % (2 * length) * (np.pi / length)
    fine = (low[:, None] * frame[None, :]) % (2 * length) * (np.pi / length)
    return [
        jnp.asarray(t.astype(np.float32))
        for t in (np.cos(coarse), np.sin(coarse), np.cos(fine), np.sin(fine))
    ]


def spectral_tables(length, rows):
    split = 32
    cos_hi, sin_hi, cos_lo, sin_lo = angle_tables(length, split)
    blocks = -(-rows // split)
    cos_hi, sin_hi = cos_hi[:blocks], sin_hi[:blocks]
    cosine = cos_hi[:, None, :] * cos_lo[None, :, :] - sin_hi[:, None, :] * sin_lo[None, :, :]
    sine = sin_hi[:, None, :] * cos_lo[None, :, :] + cos_hi[:, None, :] * sin_lo[None, :, :]
    cosine = cosine.reshape(blocks * split, length)[:rows]
    sine = sine.reshape(blocks * split, length)[:rows]
    return cosine, sine


def split_three(values):
    first = lax.reduce_precision(values, exponent_bits=8, mantissa_bits=7)
    rest = values - first
    second = lax.reduce_precision(rest, exponent_bits=8, mantissa_bits=7)
    third = rest - second
    return jnp.concatenate([first, second, third], axis=1).astype(jnp.bfloat16)


def exact_product(matrix, values):
    width = values.shape[1]
    out = jnp.dot(
        matrix.astype(jnp.bfloat16), split_three(values), preferred_element_type=jnp.float32
    )
    return out[:, :width] + out[:, width : 2 * width] + out[:, 2 * width :]


def lag_table(series, count):
    length = series.shape[0]
    half = length // 2
    width = 3 * count
    frame = jnp.arange(length, dtype=jnp.int32)
    lower = (frame[None, :] <= frame[:, None]).astype(jnp.float32)
    positions = exact_product(lower, series)
    squares = jnp.sum((positions * positions).reshape(length, 3, count), axis=1)
    cosine, sine = spectral_tables(length, half + 1)
    parity = jnp.where(frame % 2 == 0, 1.0, -1.0).astype(jnp.float32)
    both = jnp.concatenate([cosine, sine[1:]], axis=0)
    signed = jnp.concatenate([positions, positions * parity[:, None]], axis=1)
    spectrum = jnp.dot(both, signed, precision=lax.Precision.HIGHEST)
    real_part = spectrum[: half + 1]
    imag_part = jnp.concatenate([jnp.zeros((1, 2 * width), jnp.float32), spectrum[half + 1 :]], axis=0)
    power = jnp.sum((real_part * real_part + imag_part * imag_part).reshape(half + 1, 2, 3, count), axis=2)
    low_q = jnp.arange(half, dtype=jnp.int32)
    weight = jnp.where(low_q == 0, 1.0, 2.0).astype(jnp.float32) / (2 * length)
    coef = power[:half] * weight[:, None, None]
    coef = coef.at[:, 1].set(jnp.where((low_q == 0)[:, None], power[0, 1][None, :] / (2 * length), coef[:, 1]))
    sign_q = jnp.where(low_q % 2 == 0, 1.0, -1.0).astype(jnp.float32)
    coef = coef.reshape(half, 2 * count)
    coef = jnp.concatenate([coef, coef * sign_q[:, None]], axis=1)
    middle = power[half, 0] * (2.0 / (2 * length))
    table = cosine[:, :half]
    folded = jnp.dot(table, coef, precision=lax.Precision.HIGHEST)
    lag = jnp.arange(half + 1, dtype=jnp.int32)
    sign_m = jnp.where(lag % 2 == 0, 1.0, -1.0).astype(jnp.float32)[:, None]
    quarter = jnp.where(lag % 4 == 0, 1.0, jnp.where(lag % 4 == 2, -1.0, 0.0)).astype(jnp.float32)[:, None]
    near = folded[:, :count] + sign_m * folded[:, count : 2 * count] + middle[None, :] * quarter
    far = folded[:, 2 * count : 3 * count] + sign_m * folded[:, 3 * count :] + middle[None, :] * quarter
    corr = jnp.concatenate([near, jnp.flip(far[1:half], axis=0)], axis=0)
    window = (
        (frame[None, :] >= frame[:, None]).astype(jnp.float32)
        + (frame[None, :] <= (length - 1 - frame)[:, None]).astype(jnp.float32)
    )
    numer = exact_product(window, squares) - 2.0 * corr
    counts = (length - frame).astype(jnp.float32)
    return jnp.transpose(numer / counts[:, None])


def per_device(displacements):
    local_frames, _, atom_count = displacements.shape
    groups = lax.axis_size("frames")
    atom_total = atom_count * lax.axis_size("atoms")
    members = lax.axis_size("atoms")
    partial_sum = jnp.sum(displacements, axis=2).reshape(1, local_frames * 3)
    spread = jnp.broadcast_to(partial_sum, (members, local_frames * 3))
    gathered = lax.all_to_all(spread, "atoms", split_axis=0, concat_axis=0, tiled=True)
    summed = jnp.sum(gathered, axis=0).reshape(local_frames, 3)
    centred = displacements - (summed / atom_total)[:, :, None]
    count = atom_count // groups
    blocks = centred.reshape(local_frames, 3, groups, count)
    outgoing = jnp.transpose(blocks, (2, 0, 1, 3)).reshape(groups, local_frames * 3 * count)
    moved = lax.all_to_all(outgoing, "frames", split_axis=0, concat_axis=0, tiled=True)
    series = moved.reshape(groups * local_frames, 3 * count)
    return lag_table(series, count)


def solution(mesh):
    placed = (P("frames", None, "atoms"),)
    return jax.shard_map(
        per_device,
        mesh=mesh,
        in_specs=placed,
        out_specs=P(("atoms", "frames"), None),
        check_vma=False,
    )
```

```python
import numpy as np

import jax
import jax.numpy as jnp
from jax import lax
from jax.sharding import PartitionSpec as P


def angle_tables(length, split):
    frame = np.arange(length, dtype=np.int64)
    low = np.arange(split, dtype=np.int64)
    high = np.arange(length // split, dtype=np.int64) * split
    coarse = (high[:, None] * frame[None, :]) % (2 * length) * (np.pi / length)
    fine = (low[:, None] * frame[None, :]) % (2 * length) * (np.pi / length)
    return [
        jnp.asarray(t.astype(np.float32))
        for t in (np.cos(coarse), np.sin(coarse), np.cos(fine), np.sin(fine))
    ]


def spectral_tables(length, rows, anchor):
    split = 32
    blocks = rows // split
    cos_hi, sin_hi, cos_lo, sin_lo = angle_tables(length, split)
    cos_hi, sin_hi, cos_lo, sin_lo, _ = lax.optimization_barrier(
        (cos_hi[:blocks], sin_hi[:blocks], cos_lo, sin_lo, anchor)
    )
    cosine = cos_hi[:, None, :] * cos_lo[None, :, :] - sin_hi[:, None, :] * sin_lo[None, :, :]
    sine = sin_hi[:, None, :] * cos_lo[None, :, :] + cos_hi[:, None, :] * sin_lo[None, :, :]
    return cosine.reshape(rows, length), sine.reshape(rows, length)


def split_three(values):
    first = lax.reduce_precision(values, exponent_bits=8, mantissa_bits=7)
    rest = values - first
    second = lax.reduce_precision(rest, exponent_bits=8, mantissa_bits=7)
    third = rest - second
    return jnp.concatenate([first, second, third], axis=1).astype(jnp.bfloat16)


def exact_product(matrix, values):
    width = values.shape[1]
    out = jnp.dot(
        matrix.astype(jnp.bfloat16), split_three(values), preferred_element_type=jnp.float32
    )
    return out[:, :width] + out[:, width : 2 * width] + out[:, 2 * width :]


def lag_table(series, count, anchor):
    length = series.shape[0]
    half = length // 2
    width = 3 * count
    frame = jnp.arange(length, dtype=jnp.int32)
    lower = (frame[None, :] <= frame[:, None]).astype(jnp.float32)
    positions = exact_product(lower, series)
    squares = jnp.sum((positions * positions).reshape(length, 3, count), axis=1)
    cosine, sine = spectral_tables(length, half, anchor)
    parity = jnp.where(frame % 2 == 0, 1.0, -1.0).astype(jnp.float32)
    quarter_cos = jnp.where(frame % 4 == 0, 1.0, jnp.where(frame % 4 == 2, -1.0, 0.0))
    quarter_sin = jnp.where(frame % 4 == 1, 1.0, jnp.where(frame % 4 == 3, -1.0, 0.0))
    extra = jnp.stack([quarter_cos, quarter_sin]).astype(jnp.float32)
    both = jnp.concatenate([cosine, sine, extra], axis=0)
    signed = jnp.concatenate([positions, positions * parity[:, None]], axis=1)
    spectrum = jnp.dot(both, signed, precision=lax.Precision.HIGHEST)
    real_part = spectrum[:half]
    imag_part = spectrum[half : 2 * half]
    power = jnp.sum((real_part * real_part + imag_part * imag_part).reshape(half, 2, 3, count), axis=2)
    top = spectrum[2 * half :, :width]
    middle = jnp.sum((top * top).reshape(2 * 3, count), axis=0) * (2.0 / (2 * length))
    low_q = jnp.arange(half, dtype=jnp.int32)
    weight = jnp.where(low_q == 0, 1.0, 2.0).astype(jnp.float32) / (2 * length)
    coef = (power * weight[:, None, None]).reshape(half, 2 * count)
    sign_q = jnp.where(low_q % 2 == 0, 1.0, -1.0).astype(jnp.float32)
    coef = jnp.concatenate([coef, coef * sign_q[:, None]], axis=1)
    table = jnp.concatenate([cosine[:, :half], extra[:1, :half]], axis=0)
    folded = jnp.dot(table, coef, precision=lax.Precision.HIGHEST)
    lag = jnp.arange(half + 1, dtype=jnp.int32)
    sign_m = jnp.where(lag % 2 == 0, 1.0, -1.0).astype(jnp.float32)[:, None]
    quarter = jnp.where(lag % 4 == 0, 1.0, jnp.where(lag % 4 == 2, -1.0, 0.0)).astype(jnp.float32)[:, None]
    near = folded[:, :count] + sign_m * folded[:, count : 2 * count] + middle[None, :] * quarter
    far = folded[:, 2 * count : 3 * count] + sign_m * folded[:, 3 * count :] + middle[None, :] * quarter
    corr = jnp.concatenate([near, jnp.flip(far[1:half], axis=0)], axis=0)
    window = (
        (frame[None, :] >= frame[:, None]).astype(jnp.float32)
        + (frame[None, :] <= (length - 1 - frame)[:, None]).astype(jnp.float32)
    )
    numer = exact_product(window, squares) - 2.0 * corr
    counts = (length - frame).astype(jnp.float32)
    return jnp.transpose(numer / counts[:, None])


def per_device(displacements):
    local_frames, _, atom_count = displacements.shape
    groups = lax.axis_size("frames")
    atom_total = atom_count * lax.axis_size("atoms")
    members = lax.axis_size("atoms")
    partial_sum = jnp.sum(displacements, axis=2).reshape(1, local_frames * 3)
    spread = jnp.broadcast_to(partial_sum, (members, local_frames * 3))
    gathered = lax.all_to_all(spread, "atoms", split_axis=0, concat_axis=0, tiled=True)
    summed = jnp.sum(gathered, axis=0).reshape(local_frames, 3)
    centred = displacements - (summed / atom_total)[:, :, None]
    count = atom_count // groups
    blocks = centred.reshape(local_frames, 3, groups, count)
    outgoing = jnp.transpose(blocks, (2, 0, 1, 3)).reshape(groups, local_frames * 3 * count)
    moved = lax.all_to_all(outgoing, "frames", split_axis=0, concat_axis=0, tiled=True)
    series = moved.reshape(groups * local_frames, 3 * count)
    return lag_table(series, count, outgoing)


def solution(mesh):
    placed = (P("frames", None, "atoms"),)
    return jax.shard_map(
        per_device,
        mesh=mesh,
        in_specs=placed,
        out_specs=P(("atoms", "frames"), None),
        check_vma=False,
    )
```

```python
import numpy as np

import jax
import jax.numpy as jnp
from jax import lax
from jax.sharding import PartitionSpec as P


def angle_tables(length, split):
    frame = np.arange(length, dtype=np.int64)
    low = np.arange(split, dtype=np.int64)
    high = np.arange(length // split, dtype=np.int64) * split
    coarse = (high[:, None] * frame[None, :]) % (2 * length) * (np.pi / length)
    fine = (low[:, None] * frame[None, :]) % (2 * length) * (np.pi / length)
    return [
        jnp.asarray(t.astype(np.float32))
        for t in (np.cos(coarse), np.sin(coarse), np.cos(fine), np.sin(fine))
    ]


def spectral_tables(length, rows, anchor):
    split = 32
    blocks = rows // split
    cos_hi, sin_hi, cos_lo, sin_lo = angle_tables(length, split)
    cos_hi, sin_hi, cos_lo, sin_lo, _ = lax.optimization_barrier(
        (cos_hi[:blocks], sin_hi[:blocks], cos_lo, sin_lo, anchor)
    )
    cosine = cos_hi[:, None, :] * cos_lo[None, :, :] - sin_hi[:, None, :] * sin_lo[None, :, :]
    sine = sin_hi[:, None, :] * cos_lo[None, :, :] + cos_hi[:, None, :] * sin_lo[None, :, :]
    return cosine.reshape(rows, length), sine.reshape(rows, length)


def split_three(values):
    first = lax.reduce_precision(values, exponent_bits=8, mantissa_bits=7)
    rest = values - first
    second = lax.reduce_precision(rest, exponent_bits=8, mantissa_bits=7)
    third = rest - second
    return jnp.concatenate([first, second, third], axis=1).astype(jnp.bfloat16)


def exact_product(matrix, values):
    width = values.shape[1]
    out = jnp.dot(
        matrix.astype(jnp.bfloat16), split_three(values), preferred_element_type=jnp.float32
    )
    return out[:, :width] + out[:, width : 2 * width] + out[:, 2 * width :]


def lag_table(series, count, anchor):
    length = series.shape[0]
    half = length // 2
    width = 3 * count
    frame = jnp.arange(length, dtype=jnp.int32)
    lower = (frame[None, :] <= frame[:, None]).astype(jnp.float32)
    positions = exact_product(lower, series)
    squares = jnp.sum((positions * positions).reshape(length, 3, count), axis=1)
    cosine, sine = spectral_tables(length, half, anchor)
    parity = jnp.where(frame % 2 == 0, 1.0, -1.0).astype(jnp.float32)
    quarter_cos = jnp.where(frame % 4 == 0, 1.0, jnp.where(frame % 4 == 2, -1.0, 0.0))
    quarter_sin = jnp.where(frame % 4 == 1, 1.0, jnp.where(frame % 4 == 3, -1.0, 0.0))
    extra = jnp.stack([quarter_cos, quarter_sin]).astype(jnp.float32)
    both = jnp.concatenate([cosine, sine, extra], axis=0)
    signed = jnp.concatenate([positions, positions * parity[:, None]], axis=1)
    spectrum = jnp.dot(both, signed, precision=lax.Precision.HIGHEST)
    real_part = spectrum[:half]
    imag_part = spectrum[half : 2 * half]
    power = jnp.sum((real_part * real_part + imag_part * imag_part).reshape(half, 2, 3, count), axis=2)
    top = spectrum[2 * half :, :width]
    middle = jnp.sum((top * top).reshape(2 * 3, count), axis=0) * (2.0 / (2 * length))
    low_q = jnp.arange(half, dtype=jnp.int32)
    weight = jnp.where(low_q == 0, 1.0, 2.0).astype(jnp.float32) / (2 * length)
    coef = (power * weight[:, None, None]).reshape(half, 2 * count)
    sign_q = jnp.where(low_q % 2 == 0, 1.0, -1.0).astype(jnp.float32)
    coef = jnp.concatenate([coef, coef * sign_q[:, None]], axis=1)
    table = jnp.concatenate([cosine[:, :half], extra[:1, :half]], axis=0)
    folded = jnp.dot(table, coef, precision=lax.Precision.HIGHEST)
    lag = jnp.arange(half + 1, dtype=jnp.int32)
    sign_m = jnp.where(lag % 2 == 0, 1.0, -1.0).astype(jnp.float32)[:, None]
    quarter = jnp.where(lag % 4 == 0, 1.0, jnp.where(lag % 4 == 2, -1.0, 0.0)).astype(jnp.float32)[:, None]
    near = folded[:, :count] + sign_m * folded[:, count : 2 * count] + middle[None, :] * quarter
    far = folded[:, 2 * count : 3 * count] + sign_m * folded[:, 3 * count :] + middle[None, :] * quarter
    corr = jnp.concatenate([near, jnp.flip(far[1:half], axis=0)], axis=0)
    window = (
        (frame[None, :] >= frame[:, None]).astype(jnp.float32)
        + (frame[None, :] <= (length - 1 - frame)[:, None]).astype(jnp.float32)
    )
    numer = exact_product(window, squares) - 2.0 * corr
    counts = (length - frame).astype(jnp.float32)
    return jnp.transpose(numer / counts[:, None])


def per_device(displacements):
    local_frames, _, atom_count = displacements.shape
    groups = lax.axis_size(("frames_high", "frames_low"))
    atom_total = atom_count * lax.axis_size("atoms")
    members = lax.axis_size("atoms")
    partial_sum = jnp.sum(displacements, axis=2).reshape(1, local_frames * 3)
    spread = jnp.broadcast_to(partial_sum, (members, local_frames * 3))
    gathered = lax.all_to_all(spread, "atoms", split_axis=0, concat_axis=0, tiled=True)
    summed = jnp.sum(gathered, axis=0).reshape(local_frames, 3)
    centred = displacements - (summed / atom_total)[:, :, None]
    count = atom_count // groups
    blocks = centred.reshape(local_frames, 3, groups, count)
    outgoing = jnp.transpose(blocks, (2, 0, 1, 3))
    inner = lax.axis_size("frames_low")
    outer = groups // inner
    row = local_frames * 3 * count
    by_low = outgoing.reshape(outer, inner, row).transpose(1, 0, 2)
    first = lax.all_to_all(by_low, "frames_low", split_axis=0, concat_axis=0, tiled=True)
    by_high = first.transpose(1, 0, 2)
    moved = lax.all_to_all(by_high, "frames_high", split_axis=0, concat_axis=0, tiled=True)
    series = moved.reshape(groups * local_frames, 3 * count)
    return lag_table(series, count, outgoing)


def solution(mesh):
    frames, atoms = mesh.shape["frames"], mesh.shape["atoms"]
    inner = 8 if frames % 8 == 0 else 1
    split = jax.sharding.Mesh(
        mesh.devices.reshape(frames // inner, inner, atoms), ("frames_high", "frames_low", "atoms")
    )
    placed = (P(("frames_high", "frames_low"), None, "atoms"),)
    return jax.shard_map(
        per_device,
        mesh=split,
        in_specs=placed,
        out_specs=P(("atoms", "frames_high", "frames_low"), None),
        check_vma=False,
    )
```

```python
import numpy as np

import jax
import jax.numpy as jnp
from jax import lax
from jax.sharding import PartitionSpec as P


def angle_tables(length, split):
    frame = np.arange(length, dtype=np.int64)
    low = np.arange(split, dtype=np.int64)
    high = np.arange(length // split, dtype=np.int64) * split
    coarse = (high[:, None] * frame[None, :]) % (2 * length) * (np.pi / length)
    fine = (low[:, None] * frame[None, :]) % (2 * length) * (np.pi / length)
    return [
        jnp.asarray(t.astype(np.float32))
        for t in (np.cos(coarse), np.sin(coarse), np.cos(fine), np.sin(fine))
    ]


def spectral_tables(length, rows, anchor):
    split = 32
    blocks = rows // split
    cos_hi, sin_hi, cos_lo, sin_lo = angle_tables(length, split)
    cos_hi, sin_hi, cos_lo, sin_lo, _ = lax.optimization_barrier(
        (cos_hi[:blocks], sin_hi[:blocks], cos_lo, sin_lo, anchor)
    )
    cosine = cos_hi[:, None, :] * cos_lo[None, :, :] - sin_hi[:, None, :] * sin_lo[None, :, :]
    sine = sin_hi[:, None, :] * cos_lo[None, :, :] + cos_hi[:, None, :] * sin_lo[None, :, :]
    return cosine.reshape(rows, length), sine.reshape(rows, length)


def split_three(values):
    first = lax.reduce_precision(values, exponent_bits=8, mantissa_bits=7)
    rest = values - first
    second = lax.reduce_precision(rest, exponent_bits=8, mantissa_bits=7)
    third = rest - second
    return jnp.concatenate([first, second, third], axis=1).astype(jnp.bfloat16)


def exact_product(matrix, values):
    width = values.shape[1]
    out = jnp.dot(
        matrix.astype(jnp.bfloat16), split_three(values), preferred_element_type=jnp.float32
    )
    return out[:, :width] + out[:, width : 2 * width] + out[:, 2 * width :]


def lag_table(series, count, anchor):
    length = series.shape[0]
    half = length // 2
    width = 3 * count
    frame = jnp.arange(length, dtype=jnp.int32)
    lower = (frame[None, :] <= frame[:, None]).astype(jnp.float32)
    positions = exact_product(lower, series)
    squares = jnp.sum((positions * positions).reshape(length, 3, count), axis=1)
    cosine, sine = spectral_tables(length, half, anchor)
    parity = jnp.where(frame % 2 == 0, 1.0, -1.0).astype(jnp.float32)
    quarter_cos = jnp.where(frame % 4 == 0, 1.0, jnp.where(frame % 4 == 2, -1.0, 0.0))
    quarter_sin = jnp.where(frame % 4 == 1, 1.0, jnp.where(frame % 4 == 3, -1.0, 0.0))
    extra = jnp.stack([quarter_cos, quarter_sin]).astype(jnp.float32)
    both = jnp.concatenate([cosine, sine, extra], axis=0)
    signed = jnp.concatenate([positions, positions * parity[:, None]], axis=1)
    spectrum = jnp.dot(both, signed, precision=lax.Precision.HIGHEST)
    real_part = spectrum[:half]
    imag_part = spectrum[half : 2 * half]
    power = jnp.sum((real_part * real_part + imag_part * imag_part).reshape(half, 2, 3, count), axis=2)
    top = spectrum[2 * half :, :width]
    middle = jnp.sum((top * top).reshape(2 * 3, count), axis=0) * (2.0 / (2 * length))
    low_q = jnp.arange(half, dtype=jnp.int32)
    weight = jnp.where(low_q == 0, 1.0, 2.0).astype(jnp.float32) / (2 * length)
    coef = (power * weight[:, None, None]).reshape(half, 2 * count)
    sign_q = jnp.where(low_q % 2 == 0, 1.0, -1.0).astype(jnp.float32)
    coef = jnp.concatenate([coef, coef * sign_q[:, None]], axis=1)
    table = jnp.concatenate([cosine[:, :half], extra[:1, :half]], axis=0)
    folded = jnp.dot(table, coef, precision=lax.Precision.HIGHEST)
    lag = jnp.arange(half + 1, dtype=jnp.int32)
    sign_m = jnp.where(lag % 2 == 0, 1.0, -1.0).astype(jnp.float32)[:, None]
    quarter = jnp.where(lag % 4 == 0, 1.0, jnp.where(lag % 4 == 2, -1.0, 0.0)).astype(jnp.float32)[:, None]
    near = folded[:, :count] + sign_m * folded[:, count : 2 * count] + middle[None, :] * quarter
    far = folded[:, 2 * count : 3 * count] + sign_m * folded[:, 3 * count :] + middle[None, :] * quarter
    corr = jnp.concatenate([near, jnp.flip(far[1:half], axis=0)], axis=0)
    window = (
        (frame[None, :] >= frame[:, None]).astype(jnp.float32)
        + (frame[None, :] <= (length - 1 - frame)[:, None]).astype(jnp.float32)
    )
    numer = exact_product(window, squares) - 2.0 * corr
    counts = (length - frame).astype(jnp.float32)
    return jnp.transpose(numer / counts[:, None])


def per_device(displacements):
    local_frames, _, atom_count = displacements.shape
    groups = lax.axis_size("frames")
    atom_total = atom_count * lax.axis_size("atoms")
    members = lax.axis_size("atoms")
    partial_sum = jnp.sum(displacements, axis=2).reshape(1, local_frames * 3)
    spread = jnp.broadcast_to(partial_sum, (members, local_frames * 3))
    gathered = lax.all_to_all(spread, "atoms", split_axis=0, concat_axis=0, tiled=True)
    summed = jnp.sum(gathered, axis=0).reshape(local_frames, 3)
    count = atom_count // groups
    blocks = jnp.transpose(displacements.reshape(local_frames, 3, groups, count), (2, 0, 1, 3))
    outgoing = blocks - (summed / atom_total)[None, :, :, None]
    outgoing = outgoing.reshape(groups, local_frames * 3 * count)
    moved = lax.all_to_all(outgoing, "frames", split_axis=0, concat_axis=0, tiled=True)
    series = moved.reshape(groups * local_frames, 3 * count)
    return lag_table(series, count, outgoing)


def solution(mesh):
    placed = (P("frames", None, "atoms"),)
    return jax.shard_map(
        per_device,
        mesh=mesh,
        in_specs=placed,
        out_specs=P(("atoms", "frames"), None),
        check_vma=False,
    )
```

```python
import numpy as np

import jax
import jax.numpy as jnp
from jax import lax
from jax.sharding import PartitionSpec as P


def parity_tables(length):
    frame = np.arange(length // 2, dtype=np.int64)
    high = np.arange(length // 128, dtype=np.int64) * 64
    low = np.arange(2, dtype=np.int64)[:, None] + 2 * np.arange(32, dtype=np.int64)[None, :]
    coarse = (high[:, None] * frame[None, :]) % (2 * length) * (np.pi / length)
    fine = (low[:, :, None] * frame[None, None, :]) % (2 * length) * (np.pi / length)
    return [
        jnp.asarray(t.astype(np.float32))
        for t in (np.cos(coarse), np.sin(coarse), np.cos(fine), np.sin(fine))
    ]


def folded_tables(length, anchor):
    cos_hi, sin_hi, cos_lo, sin_lo = parity_tables(length)
    cos_hi, sin_hi, cos_lo, sin_lo, _ = lax.optimization_barrier(
        (cos_hi, sin_hi, cos_lo, sin_lo, anchor)
    )
    first = jnp.stack([cos_hi, sin_hi])
    second = jnp.stack([-sin_hi, cos_hi])
    rows = length // 2

    def build(order):
        lo_cos = cos_lo[jnp.array(order)]
        lo_sin = sin_lo[jnp.array(order)]
        table = first[:, :, None, :] * lo_cos[:, None, :, :] + second[:, :, None, :] * lo_sin[:, None, :, :]
        return table.reshape(rows, rows)

    return build((0, 1)), build((1, 0))


def split_three(values):
    first = lax.reduce_precision(values, exponent_bits=8, mantissa_bits=7)
    rest = values - first
    second = lax.reduce_precision(rest, exponent_bits=8, mantissa_bits=7)
    third = rest - second
    return jnp.concatenate([first, second, third], axis=1).astype(jnp.bfloat16)


def exact_product(matrix, values):
    width = values.shape[1]
    out = jnp.dot(
        matrix.astype(jnp.bfloat16), split_three(values), preferred_element_type=jnp.float32
    )
    return out[:, :width] + out[:, width : 2 * width] + out[:, 2 * width :]


def lag_table(series, count, anchor):
    length = series.shape[0]
    half = length // 2
    width = 3 * count
    frame = jnp.arange(length, dtype=jnp.int32)
    lower = (frame[None, :] <= frame[:, None]).astype(jnp.float32)
    positions = exact_product(lower, series)
    squares = jnp.sum((positions * positions).reshape(length, 3, count), axis=1)
    for_s, for_d = folded_tables(length, anchor)
    parity = jnp.where(frame % 2 == 0, 1.0, -1.0).astype(jnp.float32)
    signed = jnp.concatenate([positions, positions * parity[:, None]], axis=1)
    head_part = signed[:half]
    mirrored = jnp.concatenate([jnp.zeros((1, 2 * width), jnp.float32), jnp.flip(signed[half + 1 :], axis=0)], axis=0)
    summed_pair = head_part + mirrored
    differ_pair = head_part - mirrored
    centre = signed[half]
    out_s = jnp.dot(for_s, summed_pair, precision=lax.Precision.HIGHEST)
    out_d = jnp.dot(for_d, differ_pair, precision=lax.Precision.HIGHEST)
    quarter_rows = half // 2
    q_even = 2 * jnp.arange(quarter_rows, dtype=jnp.int32)
    centre_coef = jnp.where(q_even % 4 == 0, 1.0, -1.0).astype(jnp.float32)
    centre_coef = jnp.concatenate([centre_coef, centre_coef])
    out_s = out_s + centre_coef[:, None] * centre[None, :]
    real_part = jnp.concatenate([out_s[:quarter_rows], out_d[:quarter_rows]], axis=0)
    imag_part = jnp.concatenate([out_d[quarter_rows:], out_s[quarter_rows:]], axis=0)
    power = jnp.sum((real_part * real_part + imag_part * imag_part).reshape(half, 2, 3, count), axis=2)
    low_frame = jnp.arange(half, dtype=jnp.int32)
    quarter_cos = jnp.where(low_frame % 4 == 0, 1.0, jnp.where(low_frame % 4 == 2, -1.0, 0.0)).astype(jnp.float32)
    quarter_sin = jnp.where(low_frame % 4 == 1, 1.0, jnp.where(low_frame % 4 == 3, -1.0, 0.0)).astype(jnp.float32)
    top_real = jnp.sum(quarter_cos[:, None] * summed_pair[:, :width], axis=0) + centre[:width]
    top_imag = jnp.sum(quarter_sin[:, None] * differ_pair[:, :width], axis=0)
    middle = jnp.sum((top_real * top_real + top_imag * top_imag).reshape(3, count), axis=0) * (2.0 / (2 * length))
    low_q = jnp.concatenate([q_even, q_even + 1])
    weight = jnp.where(low_q == 0, 1.0, 2.0).astype(jnp.float32) / (2 * length)
    coef = (power * weight[:, None, None]).reshape(half, 2 * count)
    sign_q = jnp.where(low_q % 2 == 0, 1.0, -1.0).astype(jnp.float32)
    coef = jnp.concatenate([coef, coef * sign_q[:, None]], axis=1)
    cos_rows = jnp.concatenate([for_s[:quarter_rows], for_d[:quarter_rows]], axis=0)
    quarter_q = jnp.where(low_q % 4 == 0, 1.0, jnp.where(low_q % 4 == 2, -1.0, 0.0)).astype(jnp.float32)
    table = jnp.concatenate([jnp.transpose(cos_rows), quarter_q[None, :]], axis=0)
    folded = jnp.dot(table, coef, precision=lax.Precision.HIGHEST)
    lag = jnp.arange(half + 1, dtype=jnp.int32)
    sign_m = jnp.where(lag % 2 == 0, 1.0, -1.0).astype(jnp.float32)[:, None]
    quarter = jnp.where(lag % 4 == 0, 1.0, jnp.where(lag % 4 == 2, -1.0, 0.0)).astype(jnp.float32)[:, None]
    near = folded[:, :count] + sign_m * folded[:, count : 2 * count] + middle[None, :] * quarter
    far = folded[:, 2 * count : 3 * count] + sign_m * folded[:, 3 * count :] + middle[None, :] * quarter
    corr = jnp.concatenate([near, jnp.flip(far[1:half], axis=0)], axis=0)
    window = (
        (frame[None, :] >= frame[:, None]).astype(jnp.float32)
        + (frame[None, :] <= (length - 1 - frame)[:, None]).astype(jnp.float32)
    )
    numer = exact_product(window, squares) - 2.0 * corr
    counts = (length - frame).astype(jnp.float32)
    return jnp.transpose(numer / counts[:, None])


def per_device(displacements):
    local_frames, _, atom_count = displacements.shape
    groups = lax.axis_size("frames")
    atom_total = atom_count * lax.axis_size("atoms")
    members = lax.axis_size("atoms")
    partial_sum = jnp.sum(displacements, axis=2).reshape(1, local_frames * 3)
    spread = jnp.broadcast_to(partial_sum, (members, local_frames * 3))
    gathered = lax.all_to_all(spread, "atoms", split_axis=0, concat_axis=0, tiled=True)
    summed = jnp.sum(gathered, axis=0).reshape(local_frames, 3)
    count = atom_count // groups
    blocks = jnp.transpose(displacements.reshape(local_frames, 3, groups, count), (2, 0, 1, 3))
    outgoing = blocks - (summed / atom_total)[None, :, :, None]
    outgoing = outgoing.reshape(groups, local_frames * 3 * count)
    moved = lax.all_to_all(outgoing, "frames", split_axis=0, concat_axis=0, tiled=True)
    series = moved.reshape(groups * local_frames, 3 * count)
    return lag_table(series, count, outgoing)


def solution(mesh):
    placed = (P("frames", None, "atoms"),)
    return jax.shard_map(
        per_device,
        mesh=mesh,
        in_specs=placed,
        out_specs=P(("atoms", "frames"), None),
        check_vma=False,
    )
```

```python
import numpy as np

import jax
import jax.numpy as jnp
from jax import lax
from jax.sharding import PartitionSpec as P


def parity_tables(length):
    frame = np.arange(length // 2, dtype=np.int64)
    high = np.arange(length // 128, dtype=np.int64) * 64
    low = np.arange(2, dtype=np.int64)[:, None] + 2 * np.arange(32, dtype=np.int64)[None, :]
    coarse = (high[:, None] * frame[None, :]) % (2 * length) * (np.pi / length)
    fine = (low[:, :, None] * frame[None, None, :]) % (2 * length) * (np.pi / length)
    return [
        jnp.asarray(t.astype(np.float32))
        for t in (np.cos(coarse), np.sin(coarse), np.cos(fine), np.sin(fine))
    ]


def folded_tables(length, anchor):
    cos_hi, sin_hi, cos_lo, sin_lo = parity_tables(length)
    cos_swap, sin_swap = jnp.flip(cos_lo, axis=0), jnp.flip(sin_lo, axis=0)
    cos_hi, sin_hi, cos_lo, sin_lo, cos_swap, sin_swap, _ = lax.optimization_barrier(
        (cos_hi, sin_hi, cos_lo, sin_lo, cos_swap, sin_swap, anchor)
    )
    first = jnp.stack([cos_hi, sin_hi])
    second = jnp.stack([-sin_hi, cos_hi])
    rows = length // 2

    def build(lo_cos, lo_sin):
        table = first[:, :, None, :] * lo_cos[:, None, :, :] + second[:, :, None, :] * lo_sin[:, None, :, :]
        return table.reshape(rows, rows)

    return build(cos_lo, sin_lo), build(cos_swap, sin_swap)


def split_three(values):
    first = lax.reduce_precision(values, exponent_bits=8, mantissa_bits=7)
    rest = values - first
    second = lax.reduce_precision(rest, exponent_bits=8, mantissa_bits=7)
    third = rest - second
    return jnp.concatenate([first, second, third], axis=1).astype(jnp.bfloat16)


def exact_product(matrix, values):
    width = values.shape[1]
    out = jnp.dot(
        matrix.astype(jnp.bfloat16), split_three(values), preferred_element_type=jnp.float32
    )
    return out[:, :width] + out[:, width : 2 * width] + out[:, 2 * width :]


def lag_table(series, count, anchor):
    length = series.shape[0]
    half = length // 2
    width = 3 * count
    frame = jnp.arange(length, dtype=jnp.int32)
    lower = (frame[None, :] <= frame[:, None]).astype(jnp.float32)
    head_rows = frame[:half]
    mirror = ((frame[None, :] <= (length - head_rows)[:, None]) & (head_rows >= 1)[:, None]).astype(jnp.float32)
    pairs = jnp.concatenate([lower, lower[:half] + mirror, lower[:half] - mirror], axis=0)
    combined = exact_product(pairs, series)
    positions = combined[:length]
    squares = jnp.sum((positions * positions).reshape(length, 3, count), axis=1)
    for_s, for_d = folded_tables(length, anchor)
    parity = jnp.where(frame % 2 == 0, 1.0, -1.0).astype(jnp.float32)
    low_parity = parity[:half, None]
    pair_sum = combined[length : length + half]
    pair_diff = combined[length + half :]
    summed_pair = jnp.concatenate([pair_sum, pair_sum * low_parity], axis=1)
    differ_pair = jnp.concatenate([pair_diff, pair_diff * low_parity], axis=1)
    centre = jnp.concatenate([positions[half], positions[half]])
    out_s = jnp.dot(for_s, summed_pair, precision=lax.Precision.HIGHEST)
    out_d = jnp.dot(for_d, differ_pair, precision=lax.Precision.HIGHEST)
    quarter_rows = half // 2
    q_even = 2 * jnp.arange(quarter_rows, dtype=jnp.int32)
    centre_coef = jnp.where(q_even % 4 == 0, 1.0, -1.0).astype(jnp.float32)
    centre_coef = jnp.concatenate([centre_coef, centre_coef])
    out_s = out_s + centre_coef[:, None] * centre[None, :]
    real_part = jnp.concatenate([out_s[:quarter_rows], out_d[:quarter_rows]], axis=0)
    imag_part = jnp.concatenate([out_d[quarter_rows:], out_s[quarter_rows:]], axis=0)
    power = jnp.sum((real_part * real_part + imag_part * imag_part).reshape(half, 2, 3, count), axis=2)
    low_frame = jnp.arange(half, dtype=jnp.int32)
    quarter_cos = jnp.where(low_frame % 4 == 0, 1.0, jnp.where(low_frame % 4 == 2, -1.0, 0.0)).astype(jnp.float32)
    quarter_sin = jnp.where(low_frame % 4 == 1, 1.0, jnp.where(low_frame % 4 == 3, -1.0, 0.0)).astype(jnp.float32)
    top_real = jnp.sum(quarter_cos[:, None] * summed_pair[:, :width], axis=0) + centre[:width]
    top_imag = jnp.sum(quarter_sin[:, None] * differ_pair[:, :width], axis=0)
    middle = jnp.sum((top_real * top_real + top_imag * top_imag).reshape(3, count), axis=0) * (2.0 / (2 * length))
    low_q = jnp.concatenate([q_even, q_even + 1])
    weight = jnp.where(low_q == 0, 1.0, 2.0).astype(jnp.float32) / (2 * length)
    coef = (power * weight[:, None, None]).reshape(half, 2 * count)
    sign_q = jnp.where(low_q % 2 == 0, 1.0, -1.0).astype(jnp.float32)
    coef = jnp.concatenate([coef, coef * sign_q[:, None]], axis=1)
    cos_rows = jnp.concatenate([for_s[:quarter_rows], for_d[:quarter_rows]], axis=0)
    quarter_q = jnp.where(low_q % 4 == 0, 1.0, jnp.where(low_q % 4 == 2, -1.0, 0.0)).astype(jnp.float32)
    table = jnp.concatenate([jnp.transpose(cos_rows), quarter_q[None, :]], axis=0)
    folded = jnp.dot(table, coef, precision=lax.Precision.HIGHEST)
    lag = jnp.arange(half + 1, dtype=jnp.int32)
    sign_m = jnp.where(lag % 2 == 0, 1.0, -1.0).astype(jnp.float32)[:, None]
    quarter = jnp.where(lag % 4 == 0, 1.0, jnp.where(lag % 4 == 2, -1.0, 0.0)).astype(jnp.float32)[:, None]
    near = folded[:, :count] + sign_m * folded[:, count : 2 * count] + middle[None, :] * quarter
    far = folded[:, 2 * count : 3 * count] + sign_m * folded[:, 3 * count :] + middle[None, :] * quarter
    corr = jnp.concatenate([near, jnp.flip(far[1:half], axis=0)], axis=0)
    window = (
        (frame[None, :] >= frame[:, None]).astype(jnp.float32)
        + (frame[None, :] <= (length - 1 - frame)[:, None]).astype(jnp.float32)
    )
    numer = exact_product(window, squares) - 2.0 * corr
    counts = (length - frame).astype(jnp.float32)
    return jnp.transpose(numer / counts[:, None])


def per_device(displacements):
    local_frames, _, atom_count = displacements.shape
    groups = lax.axis_size("frames")
    atom_total = atom_count * lax.axis_size("atoms")
    members = lax.axis_size("atoms")
    partial_sum = jnp.sum(displacements, axis=2).reshape(1, local_frames * 3)
    spread = jnp.broadcast_to(partial_sum, (members, local_frames * 3))
    gathered = lax.all_to_all(spread, "atoms", split_axis=0, concat_axis=0, tiled=True)
    summed = jnp.sum(gathered, axis=0).reshape(local_frames, 3)
    count = atom_count // groups
    blocks = jnp.transpose(displacements.reshape(local_frames, 3, groups, count), (2, 0, 1, 3))
    outgoing = blocks - (summed / atom_total)[None, :, :, None]
    outgoing = outgoing.reshape(groups, local_frames * 3 * count)
    moved = lax.all_to_all(outgoing, "frames", split_axis=0, concat_axis=0, tiled=True)
    series = moved.reshape(groups * local_frames, 3 * count)
    return lag_table(series, count, outgoing)


def solution(mesh):
    placed = (P("frames", None, "atoms"),)
    return jax.shard_map(
        per_device,
        mesh=mesh,
        in_specs=placed,
        out_specs=P(("atoms", "frames"), None),
        check_vma=False,
    )
```

```python
import numpy as np

import jax
import jax.numpy as jnp
from jax import lax
from jax.sharding import PartitionSpec as P


def angle_tables(length, split):
    frame = np.arange(length, dtype=np.int64)
    low = np.arange(split, dtype=np.int64)
    high = np.arange(length // split, dtype=np.int64) * split
    coarse = (high[:, None] * frame[None, :]) % (2 * length) * (np.pi / length)
    fine = (low[:, None] * frame[None, :]) % (2 * length) * (np.pi / length)
    return [
        jnp.asarray(t.astype(np.float32))
        for t in (np.cos(coarse), np.sin(coarse), np.cos(fine), np.sin(fine))
    ]


def spectral_tables(length, rows, anchor):
    split = 32
    blocks = rows // split
    cos_hi, sin_hi, cos_lo, sin_lo = angle_tables(length, split)
    cos_hi, sin_hi, cos_lo, sin_lo, _ = lax.optimization_barrier(
        (cos_hi[:blocks], sin_hi[:blocks], cos_lo, sin_lo, anchor)
    )
    cosine = cos_hi[:, None, :] * cos_lo[None, :, :] - sin_hi[:, None, :] * sin_lo[None, :, :]
    sine = sin_hi[:, None, :] * cos_lo[None, :, :] + cos_hi[:, None, :] * sin_lo[None, :, :]
    return cosine.reshape(rows, length), sine.reshape(rows, length)


def split_three(values):
    first = lax.reduce_precision(values, exponent_bits=8, mantissa_bits=7)
    rest = values - first
    second = lax.reduce_precision(rest, exponent_bits=8, mantissa_bits=7)
    third = rest - second
    return jnp.concatenate([first, second, third], axis=1).astype(jnp.bfloat16)


def exact_product(matrix, values):
    width = values.shape[1]
    out = jnp.dot(
        matrix.astype(jnp.bfloat16), split_three(values), preferred_element_type=jnp.float32
    )
    return out[:, :width] + out[:, width : 2 * width] + out[:, 2 * width :]


def lag_table(series, count, anchor):
    length = series.shape[0]
    half = length // 2
    width = 3 * count
    frame = jnp.arange(length, dtype=jnp.int32)
    lower = (frame[None, :] <= frame[:, None]).astype(jnp.float32)
    positions = exact_product(lower, series)
    squares = jnp.sum((positions * positions).reshape(length, 3, count), axis=1)
    cosine, sine = spectral_tables(length, half, anchor)
    parity = jnp.where(frame % 2 == 0, 1.0, -1.0).astype(jnp.float32)
    quarter_cos = jnp.where(frame % 4 == 0, 1.0, jnp.where(frame % 4 == 2, -1.0, 0.0))
    quarter_sin = jnp.where(frame % 4 == 1, 1.0, jnp.where(frame % 4 == 3, -1.0, 0.0))
    extra = jnp.stack([quarter_cos, quarter_sin]).astype(jnp.float32)
    both = jnp.concatenate([cosine, sine, extra], axis=0)
    signed = jnp.concatenate([positions, positions * parity[:, None]], axis=1)
    spectrum = jnp.dot(both, signed, precision=lax.Precision.HIGHEST)
    real_part = spectrum[:half]
    imag_part = spectrum[half : 2 * half]
    power = jnp.sum((real_part * real_part + imag_part * imag_part).reshape(half, 2, 3, count), axis=2)
    top = spectrum[2 * half :, :width]
    middle = jnp.sum((top * top).reshape(2 * 3, count), axis=0) * (2.0 / (2 * length))
    low_q = jnp.arange(half, dtype=jnp.int32)
    weight = jnp.where(low_q == 0, 1.0, 2.0).astype(jnp.float32) / (2 * length)
    coef = (power * weight[:, None, None]).reshape(half, 2 * count)
    sign_q = jnp.where(low_q % 2 == 0, 1.0, -1.0).astype(jnp.float32)
    coef = jnp.concatenate([coef, coef * sign_q[:, None]], axis=1)
    table = jnp.concatenate([cosine[:, :half], extra[:1, :half]], axis=0)
    folded = jnp.dot(table, coef, precision=lax.Precision.HIGHEST)
    lag = jnp.arange(half + 1, dtype=jnp.int32)
    sign_m = jnp.where(lag % 2 == 0, 1.0, -1.0).astype(jnp.float32)[:, None]
    quarter = jnp.where(lag % 4 == 0, 1.0, jnp.where(lag % 4 == 2, -1.0, 0.0)).astype(jnp.float32)[:, None]
    near = folded[:, :count] + sign_m * folded[:, count : 2 * count] + middle[None, :] * quarter
    far = folded[:, 2 * count : 3 * count] + sign_m * folded[:, 3 * count :] + middle[None, :] * quarter
    corr = jnp.concatenate([near, jnp.flip(far[1:half], axis=0)], axis=0)
    window = (
        (frame[None, :] >= frame[:, None]).astype(jnp.float32)
        + (frame[None, :] <= (length - 1 - frame)[:, None]).astype(jnp.float32)
    )
    numer = exact_product(window, squares) - 2.0 * corr
    counts = (length - frame).astype(jnp.float32)
    return jnp.transpose(numer / counts[:, None])


def per_device(displacements):
    local_frames, _, atom_count = displacements.shape
    groups = lax.axis_size("frames")
    atom_total = atom_count * lax.axis_size("atoms")
    members = lax.axis_size("atoms")
    partial_sum = jnp.sum(displacements, axis=2).reshape(1, local_frames * 3)
    spread = jnp.broadcast_to(partial_sum, (members, local_frames * 3))
    gathered = lax.all_to_all(spread, "atoms", split_axis=0, concat_axis=0, tiled=True)
    summed = jnp.sum(gathered, axis=0).reshape(local_frames, 3)
    count = atom_count // groups
    blocks = jnp.transpose(displacements.reshape(local_frames, 3, groups, count), (2, 0, 1, 3))
    outgoing = blocks - (summed / atom_total)[None, :, :, None]
    half_count = count // 2
    results = []
    for part in range(2):
        piece = outgoing[..., part * half_count : (part + 1) * half_count]
        piece = piece.reshape(groups, local_frames * 3 * half_count)
        moved = lax.all_to_all(piece, "frames", split_axis=0, concat_axis=0, tiled=True)
        if results:
            moved, _ = lax.optimization_barrier((moved, results[-1]))
        series = moved.reshape(groups * local_frames, 3 * half_count)
        results.append(lag_table(series, half_count, outgoing))
    return jnp.concatenate(results, axis=0)


def solution(mesh):
    placed = (P("frames", None, "atoms"),)
    return jax.shard_map(
        per_device,
        mesh=mesh,
        in_specs=placed,
        out_specs=P(("atoms", "frames"), None),
        check_vma=False,
    )
```

```python
import numpy as np

import jax
import jax.numpy as jnp
from jax import lax
from jax.sharding import PartitionSpec as P


def angle_tables(length, split):
    frame = np.arange(length, dtype=np.int64)
    low = np.arange(split, dtype=np.int64)
    high = np.arange(length // split, dtype=np.int64) * split
    coarse = (high[:, None] * frame[None, :]) % (2 * length) * (np.pi / length)
    fine = (low[:, None] * frame[None, :]) % (2 * length) * (np.pi / length)
    return np.cos(coarse), np.sin(coarse), np.cos(fine), np.sin(fine)


def spectral_table(length, rows, anchor):
    split = 32
    blocks = rows // split
    cos_hi, sin_hi, cos_lo, sin_lo = angle_tables(length, split)
    first = np.concatenate([cos_hi[:blocks], sin_hi[:blocks]]).astype(np.float32)
    second = np.concatenate([-sin_hi[:blocks], cos_hi[:blocks]]).astype(np.float32)
    parts = [jnp.asarray(t) for t in (first, second, cos_lo.astype(np.float32), sin_lo.astype(np.float32))]
    first, second, cos_lo, sin_lo, _ = lax.optimization_barrier((*parts, anchor))
    table = first[:, None, :] * cos_lo[None, :, :] + second[:, None, :] * sin_lo[None, :, :]
    table = table.reshape(2 * rows, length)
    frame = jnp.arange(length, dtype=jnp.int32)
    both_quarters = jnp.where(frame % 4 < 2, 1.0, -1.0).astype(jnp.float32)
    row = jnp.arange(2 * rows, dtype=jnp.int32)
    return jnp.where((row == rows)[:, None], both_quarters[None, :], table)


def split_three(values):
    first = lax.reduce_precision(values, exponent_bits=8, mantissa_bits=7)
    rest = values - first
    second = lax.reduce_precision(rest, exponent_bits=8, mantissa_bits=7)
    third = rest - second
    return jnp.concatenate([first, second, third], axis=1).astype(jnp.bfloat16)


def exact_product(matrix, values):
    width = values.shape[1]
    out = jnp.dot(
        matrix.astype(jnp.bfloat16), split_three(values), preferred_element_type=jnp.float32
    )
    return out[:, :width] + out[:, width : 2 * width] + out[:, 2 * width :]


def lag_table(series, count, anchor):
    length = series.shape[0]
    half = length // 2
    width = 3 * count
    frame = jnp.arange(length, dtype=jnp.int32)
    lower = (frame[None, :] <= frame[:, None]).astype(jnp.float32)
    positions = exact_product(lower, series)
    squares = jnp.sum((positions * positions).reshape(length, 3, count), axis=1)
    table_full = spectral_table(length, half, anchor)
    parity = jnp.where(frame % 2 == 0, 1.0, -1.0).astype(jnp.float32)
    quarter_cos = jnp.where(frame % 4 == 0, 1.0, jnp.where(frame % 4 == 2, -1.0, 0.0)).astype(jnp.float32)
    signed = jnp.concatenate([positions, positions * parity[:, None]], axis=1)
    spectrum = jnp.dot(table_full, signed, precision=lax.Precision.HIGHEST)
    real_part = spectrum[:half]
    low_rows = jnp.arange(half, dtype=jnp.int32)
    imag_part = jnp.where((low_rows == 0)[:, None], 0.0, spectrum[half:])
    power = jnp.sum((real_part * real_part + imag_part * imag_part).reshape(half, 2, 3, count), axis=2)
    plus, minus = spectrum[half, :width], spectrum[half, width:]
    middle = jnp.sum((0.5 * (plus * plus + minus * minus)).reshape(3, count), axis=0) * (2.0 / (2 * length))
    low_q = jnp.arange(half, dtype=jnp.int32)
    weight = jnp.where(low_q == 0, 1.0, 2.0).astype(jnp.float32) / (2 * length)
    coef = (power * weight[:, None, None]).reshape(half, 2 * count)
    sign_q = jnp.where(low_q % 2 == 0, 1.0, -1.0).astype(jnp.float32)
    coef = jnp.concatenate([coef, coef * sign_q[:, None]], axis=1)
    table = jnp.concatenate([table_full[:half, :half], quarter_cos[None, :half]], axis=0)
    folded = jnp.dot(table, coef, precision=lax.Precision.HIGHEST)
    lag = jnp.arange(half + 1, dtype=jnp.int32)
    sign_m = jnp.where(lag % 2 == 0, 1.0, -1.0).astype(jnp.float32)[:, None]
    quarter = jnp.where(lag % 4 == 0, 1.0, jnp.where(lag % 4 == 2, -1.0, 0.0)).astype(jnp.float32)[:, None]
    near = folded[:, :count] + sign_m * folded[:, count : 2 * count] + middle[None, :] * quarter
    far = folded[:, 2 * count : 3 * count] + sign_m * folded[:, 3 * count :] + middle[None, :] * quarter
    corr = jnp.concatenate([near, jnp.flip(far[1:half], axis=0)], axis=0)
    window = (
        (frame[None, :] >= frame[:, None]).astype(jnp.float32)
        + (frame[None, :] <= (length - 1 - frame)[:, None]).astype(jnp.float32)
    )
    numer = exact_product(window, squares) - 2.0 * corr
    counts = (length - frame).astype(jnp.float32)
    return jnp.transpose(numer / counts[:, None])


def per_device(displacements):
    local_frames, _, atom_count = displacements.shape
    groups = lax.axis_size("frames")
    atom_total = atom_count * lax.axis_size("atoms")
    members = lax.axis_size("atoms")
    partial_sum = jnp.sum(displacements, axis=2).reshape(1, local_frames * 3)
    spread = jnp.broadcast_to(partial_sum, (members, local_frames * 3))
    gathered = lax.all_to_all(spread, "atoms", split_axis=0, concat_axis=0, tiled=True)
    summed = jnp.sum(gathered, axis=0).reshape(local_frames, 3)
    count = atom_count // groups
    blocks = jnp.transpose(displacements.reshape(local_frames, 3, groups, count), (2, 0, 1, 3))
    outgoing = blocks - (summed / atom_total)[None, :, :, None]
    outgoing = outgoing.reshape(groups, local_frames * 3 * count)
    moved = lax.all_to_all(outgoing, "frames", split_axis=0, concat_axis=0, tiled=True)
    series = moved.reshape(groups * local_frames, 3 * count)
    return lag_table(series, count, outgoing)


def solution(mesh):
    placed = (P("frames", None, "atoms"),)
    return jax.shard_map(
        per_device,
        mesh=mesh,
        in_specs=placed,
        out_specs=P(("atoms", "frames"), None),
        check_vma=False,
    )
```

```python
import numpy as np

import jax
import jax.numpy as jnp
from jax import lax
from jax.sharding import PartitionSpec as P


def angle_tables(length, split):
    frame = np.arange(length, dtype=np.int64)
    low = np.arange(split, dtype=np.int64)
    high = np.arange(length // split, dtype=np.int64) * split
    coarse = (high[:, None] * frame[None, :]) % (2 * length) * (np.pi / length)
    fine = (low[:, None] * frame[None, :]) % (2 * length) * (np.pi / length)
    return np.cos(coarse), np.sin(coarse), np.cos(fine), np.sin(fine)


def table_parts(length, rows):
    split = 32
    blocks = rows // split
    cos_hi, sin_hi, cos_lo, sin_lo = angle_tables(length, split)
    first = np.concatenate([cos_hi[:blocks], sin_hi[:blocks]]).astype(np.float32)
    second = np.concatenate([-sin_hi[:blocks], cos_hi[:blocks]]).astype(np.float32)
    return [jnp.asarray(t) for t in (first, second, cos_lo.astype(np.float32), sin_lo.astype(np.float32))]


def spectral_table(length, rows, parts):
    first, second, cos_lo, sin_lo = parts
    table = first[:, None, :] * cos_lo[None, :, :] + second[:, None, :] * sin_lo[None, :, :]
    table = table.reshape(2 * rows, length)
    frame = jnp.arange(length, dtype=jnp.int32)
    both_quarters = jnp.where(frame % 4 < 2, 1.0, -1.0).astype(jnp.float32)
    row = jnp.arange(2 * rows, dtype=jnp.int32)
    return jnp.where((row == rows)[:, None], both_quarters[None, :], table)


def split_three(values):
    first = lax.reduce_precision(values, exponent_bits=8, mantissa_bits=7)
    rest = values - first
    second = lax.reduce_precision(rest, exponent_bits=8, mantissa_bits=7)
    third = rest - second
    return jnp.concatenate([first, second, third], axis=1).astype(jnp.bfloat16)


def exact_product(matrix, values):
    width = values.shape[1]
    out = jnp.dot(
        matrix.astype(jnp.bfloat16), split_three(values), preferred_element_type=jnp.float32
    )
    return out[:, :width] + out[:, width : 2 * width] + out[:, 2 * width :]


def lag_table(series, count, parts):
    length = series.shape[0]
    half = length // 2
    width = 3 * count
    frame = jnp.arange(length, dtype=jnp.int32)
    lower = (frame[None, :] <= frame[:, None]).astype(jnp.float32)
    positions = exact_product(lower, series)
    squares = jnp.sum((positions * positions).reshape(length, 3, count), axis=1)
    table_full = spectral_table(length, half, parts)
    parity = jnp.where(frame % 2 == 0, 1.0, -1.0).astype(jnp.float32)
    quarter_cos = jnp.where(frame % 4 == 0, 1.0, jnp.where(frame % 4 == 2, -1.0, 0.0)).astype(jnp.float32)
    signed = jnp.concatenate([positions, positions * parity[:, None]], axis=1)
    spectrum = jnp.dot(table_full, signed, precision=lax.Precision.HIGHEST)
    real_part = spectrum[:half]
    low_rows = jnp.arange(half, dtype=jnp.int32)
    imag_part = jnp.where((low_rows == 0)[:, None], 0.0, spectrum[half:])
    power = jnp.sum((real_part * real_part + imag_part * imag_part).reshape(half, 2, 3, count), axis=2)
    plus, minus = spectrum[half, :width], spectrum[half, width:]
    middle = jnp.sum((0.5 * (plus * plus + minus * minus)).reshape(3, count), axis=0) * (2.0 / (2 * length))
    low_q = jnp.arange(half, dtype=jnp.int32)
    weight = jnp.where(low_q == 0, 1.0, 2.0).astype(jnp.float32) / (2 * length)
    coef = (power * weight[:, None, None]).reshape(half, 2 * count)
    sign_q = jnp.where(low_q % 2 == 0, 1.0, -1.0).astype(jnp.float32)
    coef = jnp.concatenate([coef, coef * sign_q[:, None]], axis=1)
    table = jnp.concatenate([table_full[:half, :half], quarter_cos[None, :half]], axis=0)
    folded = jnp.dot(table, coef, precision=lax.Precision.HIGHEST)
    lag = jnp.arange(half + 1, dtype=jnp.int32)
    sign_m = jnp.where(lag % 2 == 0, 1.0, -1.0).astype(jnp.float32)[:, None]
    quarter = jnp.where(lag % 4 == 0, 1.0, jnp.where(lag % 4 == 2, -1.0, 0.0)).astype(jnp.float32)[:, None]
    near = folded[:, :count] + sign_m * folded[:, count : 2 * count] + middle[None, :] * quarter
    far = folded[:, 2 * count : 3 * count] + sign_m * folded[:, 3 * count :] + middle[None, :] * quarter
    corr = jnp.concatenate([near, jnp.flip(far[1:half], axis=0)], axis=0)
    window = (
        (frame[None, :] >= frame[:, None]).astype(jnp.float32)
        + (frame[None, :] <= (length - 1 - frame)[:, None]).astype(jnp.float32)
    )
    numer = exact_product(window, squares) - 2.0 * corr
    counts = (length - frame).astype(jnp.float32)
    return jnp.transpose(numer / counts[:, None])


def per_device(displacements):
    local_frames, _, atom_count = displacements.shape
    groups = lax.axis_size("frames")
    atom_total = atom_count * lax.axis_size("atoms")
    members = lax.axis_size("atoms")
    partial_sum = jnp.sum(displacements, axis=2).reshape(1, local_frames * 3)
    spread = jnp.broadcast_to(partial_sum, (members, local_frames * 3))
    gathered = lax.all_to_all(spread, "atoms", split_axis=0, concat_axis=0, tiled=True)
    summed = jnp.sum(gathered, axis=0).reshape(local_frames, 3)
    count = atom_count // groups
    blocks = jnp.transpose(displacements.reshape(local_frames, 3, groups, count), (2, 0, 1, 3))
    outgoing = blocks - (summed / atom_total)[None, :, :, None]
    outgoing = outgoing.reshape(groups, local_frames * 3 * count)
    length = local_frames * groups
    *parts, outgoing = lax.optimization_barrier((*table_parts(length, length // 2), outgoing))
    moved = lax.all_to_all(outgoing, "frames", split_axis=0, concat_axis=0, tiled=True)
    series = moved.reshape(length, 3 * count)
    return lag_table(series, count, parts)


def solution(mesh):
    placed = (P("frames", None, "atoms"),)
    return jax.shard_map(
        per_device,
        mesh=mesh,
        in_specs=placed,
        out_specs=P(("atoms", "frames"), None),
        check_vma=False,
    )
```

```python
import numpy as np

import jax
import jax.numpy as jnp
from jax import lax
from jax.sharding import PartitionSpec as P


def angle_tables(length, split):
    frame = np.arange(length, dtype=np.int64)
    low = np.arange(split, dtype=np.int64)
    high = np.arange(length // split, dtype=np.int64) * split
    coarse = (high[:, None] * frame[None, :]) % (2 * length) * (np.pi / length)
    fine = (low[:, None] * frame[None, :]) % (2 * length) * (np.pi / length)
    return np.cos(coarse), np.sin(coarse), np.cos(fine), np.sin(fine)


def table_parts(length, rows):
    split = 32
    blocks = rows // split
    cos_hi, sin_hi, cos_lo, sin_lo = angle_tables(length, split)
    first = np.concatenate([cos_hi[:blocks], sin_hi[:blocks]]).astype(np.float32)
    second = np.concatenate([-sin_hi[:blocks], cos_hi[:blocks]]).astype(np.float32)
    return [jnp.asarray(t) for t in (first, second, cos_lo.astype(np.float32), sin_lo.astype(np.float32))]


def spectral_table(length, rows, parts):
    first, second, cos_lo, sin_lo = parts
    table = first[:, None, :] * cos_lo[None, :, :] + second[:, None, :] * sin_lo[None, :, :]
    table = table.reshape(2 * rows, length)
    frame = jnp.arange(length, dtype=jnp.int32)
    both_quarters = jnp.where(frame % 4 < 2, 1.0, -1.0).astype(jnp.float32)
    row = jnp.arange(2 * rows, dtype=jnp.int32)
    return jnp.where((row == rows)[:, None], both_quarters[None, :], table)


def split_three(values):
    first = lax.reduce_precision(values, exponent_bits=8, mantissa_bits=7)
    rest = values - first
    second = lax.reduce_precision(rest, exponent_bits=8, mantissa_bits=7)
    third = rest - second
    return jnp.concatenate([first, second, third], axis=1).astype(jnp.bfloat16)


def exact_product(matrix, values):
    width = values.shape[1]
    out = jnp.dot(
        matrix.astype(jnp.bfloat16), split_three(values), preferred_element_type=jnp.float32
    )
    return out[:, :width] + out[:, width : 2 * width] + out[:, 2 * width :]


def lag_table(series, count, parts):
    length = series.shape[0]
    half = length // 2
    width = 3 * count
    frame = jnp.arange(length, dtype=jnp.int32)
    lower = (frame[None, :] <= frame[:, None]).astype(jnp.float32)
    positions = exact_product(lower, series)
    squares = jnp.sum((positions * positions).reshape(length, 3, count), axis=1)
    table_full = spectral_table(length, half, parts)
    steps = np.arange(length)
    parity = jnp.asarray(np.where(steps % 2 == 0, 1.0, -1.0).astype(np.float32))
    quarter_cos = np.where(steps % 4 == 0, 1.0, np.where(steps % 4 == 2, -1.0, 0.0)).astype(np.float32)
    signed = jnp.concatenate([positions, positions * parity[:, None]], axis=1)
    spectrum = jnp.dot(table_full, signed, precision=lax.Precision.HIGHEST)
    real_part = spectrum[:half]
    imag_part = spectrum[half:] * jnp.asarray((steps[:half] != 0).astype(np.float32))[:, None]
    power = jnp.sum((real_part * real_part + imag_part * imag_part).reshape(half, 2, 3, count), axis=2)
    plus, minus = spectrum[half, :width], spectrum[half, width:]
    middle = jnp.sum((0.5 * (plus * plus + minus * minus)).reshape(3, count), axis=0) * (2.0 / (2 * length))
    weight = jnp.asarray((np.where(steps[:half] == 0, 1.0, 2.0) / (2 * length)).astype(np.float32))
    coef = (power * weight[:, None, None]).reshape(half, 2 * count)
    sign_q = parity[:half]
    coef = jnp.concatenate([coef, coef * sign_q[:, None]], axis=1)
    table = jnp.concatenate([table_full[:half, :half], jnp.asarray(quarter_cos[None, :half])], axis=0)
    folded = jnp.dot(table, coef, precision=lax.Precision.HIGHEST)
    sign_m = parity[: half + 1, None]
    quarter = jnp.asarray(quarter_cos[: half + 1, None])
    near = folded[:, :count] + sign_m * folded[:, count : 2 * count] + middle[None, :] * quarter
    far = folded[:, 2 * count : 3 * count] + sign_m * folded[:, 3 * count :] + middle[None, :] * quarter
    corr = jnp.concatenate([near, jnp.flip(far[1:half], axis=0)], axis=0)
    window = (
        (frame[None, :] >= frame[:, None]).astype(jnp.float32)
        + (frame[None, :] <= (length - 1 - frame)[:, None]).astype(jnp.float32)
    )
    numer = exact_product(window, squares) - 2.0 * corr
    counts = jnp.asarray((length - steps).astype(np.float32))
    return jnp.transpose(numer / counts[:, None])


def per_device(displacements):
    local_frames, _, atom_count = displacements.shape
    groups = lax.axis_size("frames")
    atom_total = atom_count * lax.axis_size("atoms")
    members = lax.axis_size("atoms")
    partial_sum = jnp.sum(displacements, axis=2).reshape(1, local_frames * 3)
    spread = jnp.broadcast_to(partial_sum, (members, local_frames * 3))
    gathered = lax.all_to_all(spread, "atoms", split_axis=0, concat_axis=0, tiled=True)
    summed = jnp.sum(gathered, axis=0).reshape(local_frames, 3)
    count = atom_count // groups
    blocks = jnp.transpose(displacements.reshape(local_frames, 3, groups, count), (2, 0, 1, 3))
    outgoing = blocks - (summed / atom_total)[None, :, :, None]
    outgoing = outgoing.reshape(groups, local_frames * 3 * count)
    length = local_frames * groups
    *parts, outgoing = lax.optimization_barrier((*table_parts(length, length // 2), outgoing))
    moved = lax.all_to_all(outgoing, "frames", split_axis=0, concat_axis=0, tiled=True)
    series = moved.reshape(length, 3 * count)
    return lag_table(series, count, parts)


def solution(mesh):
    placed = (P("frames", None, "atoms"),)
    return jax.shard_map(
        per_device,
        mesh=mesh,
        in_specs=placed,
        out_specs=P(("atoms", "frames"), None),
        check_vma=False,
    )
```

```python
import numpy as np

import jax
import jax.numpy as jnp
from jax import lax
from jax.sharding import PartitionSpec as P


def angle_tables(length, split):
    frame = np.arange(length, dtype=np.int64)
    low = np.arange(split, dtype=np.int64)
    high = np.arange(length // split, dtype=np.int64) * split
    coarse = (high[:, None] * frame[None, :]) % (2 * length) * (np.pi / length)
    fine = (low[:, None] * frame[None, :]) % (2 * length) * (np.pi / length)
    return np.cos(coarse), np.sin(coarse), np.cos(fine), np.sin(fine)


def table_parts(length, rows):
    split = 32
    blocks = rows // split
    cos_hi, sin_hi, cos_lo, sin_lo = angle_tables(length, split)
    first = np.concatenate([cos_hi[:blocks], sin_hi[:blocks]]).astype(np.float32)
    second = np.concatenate([-sin_hi[:blocks], cos_hi[:blocks]]).astype(np.float32)
    return [jnp.asarray(t) for t in (first, second, cos_lo.astype(np.float32), sin_lo.astype(np.float32))]


def spectral_table(length, rows, parts):
    first, second, cos_lo, sin_lo = parts
    table = first[:, None, :] * cos_lo[None, :, :] + second[:, None, :] * sin_lo[None, :, :]
    table = table.reshape(2 * rows, length)
    frame = jnp.arange(length, dtype=jnp.int32)
    both_quarters = jnp.where(frame % 4 < 2, 1.0, -1.0).astype(jnp.float32)
    row = jnp.arange(2 * rows, dtype=jnp.int32)
    return jnp.where((row == rows)[:, None], both_quarters[None, :], table)


def split_three(values):
    first = lax.reduce_precision(values, exponent_bits=8, mantissa_bits=7)
    rest = values - first
    second = lax.reduce_precision(rest, exponent_bits=8, mantissa_bits=7)
    third = rest - second
    return jnp.concatenate([first, second, third], axis=1).astype(jnp.bfloat16)


def exact_product(matrix, values):
    width = values.shape[1]
    out = jnp.dot(
        matrix.astype(jnp.bfloat16), split_three(values), preferred_element_type=jnp.float32
    )
    return out[:, :width] + out[:, width : 2 * width] + out[:, 2 * width :]


def lag_table(series, count, parts):
    length = series.shape[0]
    half = length // 2
    width = 3 * count
    frame = jnp.arange(length, dtype=jnp.int32)
    lower = (frame[None, :] <= frame[:, None]).astype(jnp.float32)
    positions = exact_product(lower, series)
    squares = jnp.sum((positions * positions).reshape(length, 3, count), axis=1)
    table_full = spectral_table(length, half, parts)
    steps = np.arange(length)
    parity = jnp.asarray(np.where(steps % 2 == 0, 1.0, -1.0).astype(np.float32))
    quarter_cos = np.where(steps % 4 == 0, 1.0, np.where(steps % 4 == 2, -1.0, 0.0)).astype(np.float32)
    signed = jnp.concatenate([positions, positions * parity[:, None]], axis=1)
    spectrum = jnp.dot(table_full, signed, precision=lax.Precision.HIGHEST)
    real_part = spectrum[:half]
    imag_part = spectrum[half:] * jnp.asarray((steps[:half] != 0).astype(np.float32))[:, None]
    power = jnp.sum((real_part * real_part + imag_part * imag_part).reshape(half, 2, 3, count), axis=2)
    plus, minus = spectrum[half, :width], spectrum[half, width:]
    middle = jnp.sum((0.5 * (plus * plus + minus * minus)).reshape(3, count), axis=0) * (2.0 / (2 * length))
    weight = jnp.asarray((np.where(steps[:half] == 0, 1.0, 2.0) / (2 * length)).astype(np.float32))
    coef = (power * weight[:, None, None]).reshape(half, 2 * count)
    sign_q = parity[:half]
    coef = jnp.concatenate([coef, coef * sign_q[:, None]], axis=1)
    table = jnp.concatenate([table_full[:half, :half], jnp.asarray(quarter_cos[None, :half])], axis=0)
    folded = jnp.dot(table, coef, precision=lax.Precision.HIGHEST)
    sign_m = parity[: half + 1, None]
    quarter = jnp.asarray(quarter_cos[: half + 1, None])
    near = folded[:, :count] + sign_m * folded[:, count : 2 * count] + middle[None, :] * quarter
    far = folded[:, 2 * count : 3 * count] + sign_m * folded[:, 3 * count :] + middle[None, :] * quarter
    corr = jnp.concatenate([near, jnp.flip(far[1:half], axis=0)], axis=0)
    window = (
        (frame[None, :] >= frame[:, None]).astype(jnp.float32)
        + (frame[None, :] <= (length - 1 - frame)[:, None]).astype(jnp.float32)
    )
    numer = exact_product(window, squares) - 2.0 * corr
    counts = jnp.asarray((length - steps).astype(np.float32))
    return jnp.transpose(numer / counts[:, None])


def per_device(displacements):
    local_frames, _, atom_count = displacements.shape
    groups = lax.axis_size("frames")
    atom_total = atom_count * lax.axis_size("atoms")
    count = atom_count // groups
    length = local_frames * groups
    blocks = jnp.transpose(displacements.reshape(local_frames, 3, groups, count), (2, 0, 1, 3))
    blocks = blocks.reshape(groups, local_frames * 3 * count)
    *parts, blocks = lax.optimization_barrier((*table_parts(length, length // 2), blocks))
    moved = lax.all_to_all(blocks, "frames", split_axis=0, concat_axis=0, tiled=True)
    members = lax.axis_size("atoms")
    partial_sum = jnp.sum(displacements, axis=2).reshape(1, local_frames * 3)
    spread = jnp.broadcast_to(partial_sum, (members, local_frames * 3))
    spread, moved = lax.optimization_barrier((spread, moved))
    gathered = lax.all_to_all(spread, "atoms", split_axis=0, concat_axis=0, tiled=True)
    drift = jnp.sum(gathered, axis=0, keepdims=True) / atom_total
    everywhere = lax.all_to_all(
        jnp.broadcast_to(drift, (groups, local_frames * 3)), "frames", split_axis=0, concat_axis=0, tiled=True
    )
    raw = moved.reshape(groups, local_frames, 3, count)
    series = (raw - everywhere.reshape(groups, local_frames, 3, 1)).reshape(length, 3 * count)
    return lag_table(series, count, parts)


def solution(mesh):
    placed = (P("frames", None, "atoms"),)
    return jax.shard_map(
        per_device,
        mesh=mesh,
        in_specs=placed,
        out_specs=P(("atoms", "frames"), None),
        check_vma=False,
    )
```

```python
import numpy as np

import jax
import jax.numpy as jnp
from jax import lax
from jax.sharding import PartitionSpec as P


def angle_tables(length, split):
    frame = np.arange(length, dtype=np.int64)
    low = np.arange(split, dtype=np.int64)
    high = np.arange(length // split, dtype=np.int64) * split
    coarse = (high[:, None] * frame[None, :]) % (2 * length) * (np.pi / length)
    fine = (low[:, None] * frame[None, :]) % (2 * length) * (np.pi / length)
    return np.cos(coarse), np.sin(coarse), np.cos(fine), np.sin(fine)


def table_parts(length, rows):
    split = 32
    blocks = rows // split
    cos_hi, sin_hi, cos_lo, sin_lo = angle_tables(length, split)
    first = np.concatenate([cos_hi[:blocks], sin_hi[:blocks]]).astype(np.float32)
    second = np.concatenate([-sin_hi[:blocks], cos_hi[:blocks]]).astype(np.float32)
    return [jnp.asarray(t) for t in (first, second, cos_lo.astype(np.float32), sin_lo.astype(np.float32))]


def spectral_table(length, rows, parts):
    first, second, cos_lo, sin_lo = parts
    table = first[:, None, :] * cos_lo[None, :, :] + second[:, None, :] * sin_lo[None, :, :]
    table = table.reshape(2 * rows, length)
    frame = jnp.arange(length, dtype=jnp.int32)
    both_quarters = jnp.where(frame % 4 < 2, 1.0, -1.0).astype(jnp.float32)
    row = jnp.arange(2 * rows, dtype=jnp.int32)
    return jnp.where((row == rows)[:, None], both_quarters[None, :], table)


def split_three(values):
    first = lax.reduce_precision(values, exponent_bits=8, mantissa_bits=7)
    rest = values - first
    second = lax.reduce_precision(rest, exponent_bits=8, mantissa_bits=7)
    third = rest - second
    return jnp.concatenate([first, second, third], axis=1).astype(jnp.bfloat16)


def exact_product(matrix, values):
    width = values.shape[1]
    out = jnp.dot(
        matrix.astype(jnp.bfloat16), split_three(values), preferred_element_type=jnp.float32
    )
    return out[:, :width] + out[:, width : 2 * width] + out[:, 2 * width :]


def lag_table(series, count, parts):
    length = series.shape[0]
    half = length // 2
    width = 3 * count
    frame = jnp.arange(length, dtype=jnp.int32)
    lower = (frame[None, :] <= frame[:, None]).astype(jnp.float32)
    positions = exact_product(lower, series)
    squares = jnp.sum((positions * positions).reshape(length, 3, count), axis=1)
    table_full = spectral_table(length, half, parts)
    steps = np.arange(length)
    parity = jnp.asarray(np.where(steps % 2 == 0, 1.0, -1.0).astype(np.float32))
    quarter_cos = np.where(steps % 4 == 0, 1.0, np.where(steps % 4 == 2, -1.0, 0.0)).astype(np.float32)
    signed = jnp.concatenate([positions, positions * parity[:, None]], axis=1)
    spectrum = jnp.dot(table_full, signed, precision=lax.Precision.HIGHEST)
    real_part = spectrum[:half]
    imag_part = spectrum[half:] * jnp.asarray((steps[:half] != 0).astype(np.float32))[:, None]
    power = jnp.sum((real_part * real_part + imag_part * imag_part).reshape(half, 2, 3, count), axis=2)
    plus, minus = spectrum[half, :width], spectrum[half, width:]
    middle = jnp.sum((0.5 * (plus * plus + minus * minus)).reshape(3, count), axis=0) * (2.0 / (2 * length))
    weight = jnp.asarray((np.where(steps[:half] == 0, 1.0, 2.0) / (2 * length)).astype(np.float32))
    coef = (power * weight[:, None, None]).reshape(half, 2 * count)
    folded = lax.dot_general(
        table_full[:half], coef, (((0,), (0,)), ((), ())), precision=lax.Precision.HIGHEST
    )
    corr = (
        folded[:, :count]
        + parity[:, None] * folded[:, count:]
        + middle[None, :] * jnp.asarray(quarter_cos[:, None])
    )
    window = (
        (frame[None, :] >= frame[:, None]).astype(jnp.float32)
        + (frame[None, :] <= (length - 1 - frame)[:, None]).astype(jnp.float32)
    )
    numer = exact_product(window, squares) - 2.0 * corr
    counts = jnp.asarray((length - steps).astype(np.float32))
    return jnp.transpose(numer / counts[:, None])


def per_device(displacements):
    local_frames, _, atom_count = displacements.shape
    groups = lax.axis_size("frames")
    atom_total = atom_count * lax.axis_size("atoms")
    members = lax.axis_size("atoms")
    partial_sum = jnp.sum(displacements, axis=2).reshape(1, local_frames * 3)
    spread = jnp.broadcast_to(partial_sum, (members, local_frames * 3))
    gathered = lax.all_to_all(spread, "atoms", split_axis=0, concat_axis=0, tiled=True)
    summed = jnp.sum(gathered, axis=0).reshape(local_frames, 3)
    count = atom_count // groups
    blocks = jnp.transpose(displacements.reshape(local_frames, 3, groups, count), (2, 0, 1, 3))
    outgoing = blocks - (summed / atom_total)[None, :, :, None]
    outgoing = outgoing.reshape(groups, local_frames * 3 * count)
    length = local_frames * groups
    *parts, outgoing = lax.optimization_barrier((*table_parts(length, length // 2), outgoing))
    moved = lax.all_to_all(outgoing, "frames", split_axis=0, concat_axis=0, tiled=True)
    series = moved.reshape(length, 3 * count)
    return lag_table(series, count, parts)


def solution(mesh):
    placed = (P("frames", None, "atoms"),)
    return jax.shard_map(
        per_device,
        mesh=mesh,
        in_specs=placed,
        out_specs=P(("atoms", "frames"), None),
        check_vma=False,
    )
```

```python
import numpy as np

import jax
import jax.numpy as jnp
from jax import lax
from jax.sharding import PartitionSpec as P


def angle_tables(length, split):
    frame = np.arange(length, dtype=np.int64)
    low = np.arange(split, dtype=np.int64)
    high = np.arange(length // split, dtype=np.int64) * split
    coarse = (high[:, None] * frame[None, :]) % (2 * length) * (np.pi / length)
    fine = (low[:, None] * frame[None, :]) % (2 * length) * (np.pi / length)
    return np.cos(coarse), np.sin(coarse), np.cos(fine), np.sin(fine)


def table_parts(length, rows):
    split = 32
    blocks = rows // split
    cos_hi, sin_hi, cos_lo, sin_lo = angle_tables(length, split)
    first = np.concatenate([cos_hi[:blocks], sin_hi[:blocks]]).astype(np.float32)
    second = np.concatenate([-sin_hi[:blocks], cos_hi[:blocks]]).astype(np.float32)
    return [jnp.asarray(t) for t in (first, second, cos_lo.astype(np.float32), sin_lo.astype(np.float32))]


def spectral_table(length, rows, parts):
    first, second, cos_lo, sin_lo = parts
    table = first[:, None, :] * cos_lo[None, :, :] + second[:, None, :] * sin_lo[None, :, :]
    table = table.reshape(2 * rows, length)
    frame = jnp.arange(length, dtype=jnp.int32)
    both_quarters = jnp.where(frame % 4 < 2, 1.0, -1.0).astype(jnp.float32)
    row = jnp.arange(2 * rows, dtype=jnp.int32)
    return jnp.where((row == rows)[:, None], both_quarters[None, :], table)


def split_three(values):
    first = lax.reduce_precision(values, exponent_bits=8, mantissa_bits=7)
    rest = values - first
    second = lax.reduce_precision(rest, exponent_bits=8, mantissa_bits=7)
    third = rest - second
    return jnp.concatenate([first, second, third], axis=1).astype(jnp.bfloat16)


def exact_product(matrix, values):
    width = values.shape[1]
    out = jnp.dot(
        matrix.astype(jnp.bfloat16), split_three(values), preferred_element_type=jnp.float32
    )
    return out[:, :width] + out[:, width : 2 * width] + out[:, 2 * width :]


def lag_table(series, count, parts):
    length = series.shape[0]
    half = length // 2
    width = 3 * count
    frame = jnp.arange(length, dtype=jnp.int32)
    lower = (frame[None, :] <= frame[:, None]).astype(jnp.float32)
    positions = exact_product(lower, series)
    squares = jnp.sum((positions * positions).reshape(length, 3, count), axis=1)
    table_full = spectral_table(length, half, parts)
    steps = np.arange(length)
    parity = jnp.asarray(np.where(steps % 2 == 0, 1.0, -1.0).astype(np.float32))
    quarter_cos = np.where(steps % 4 == 0, 1.0, np.where(steps % 4 == 2, -1.0, 0.0)).astype(np.float32)
    signed = jnp.concatenate([positions, positions * parity[:, None]], axis=1)
    spectrum = jnp.dot(table_full, signed, precision=lax.Precision.HIGHEST)
    real_part = spectrum[:half]
    imag_part = spectrum[half:] * jnp.asarray((steps[:half] != 0).astype(np.float32))[:, None]
    power = jnp.sum((real_part * real_part + imag_part * imag_part).reshape(half, 2, 3, count), axis=2)
    plus, minus = spectrum[half, :width], spectrum[half, width:]
    middle = jnp.sum((0.5 * (plus * plus + minus * minus)).reshape(3, count), axis=0) * (2.0 / (2 * length))
    weight = jnp.asarray((np.where(steps[:half] == 0, 1.0, 2.0) / (2 * length)).astype(np.float32))
    coef = (power * weight[:, None, None]).reshape(half, 2 * count)
    sign_q = parity[:half]
    coef = jnp.concatenate([coef, coef * sign_q[:, None]], axis=1)
    table = jnp.concatenate([table_full[:half, :half], jnp.asarray(quarter_cos[None, :half])], axis=0)
    folded = jnp.dot(table, coef, precision=lax.Precision.HIGHEST)
    sign_m = parity[: half + 1, None]
    quarter = jnp.asarray(quarter_cos[: half + 1, None])
    near = folded[:, :count] + sign_m * folded[:, count : 2 * count] + middle[None, :] * quarter
    far = folded[:, 2 * count : 3 * count] + sign_m * folded[:, 3 * count :] + middle[None, :] * quarter
    corr = jnp.concatenate([near, jnp.flip(far[1:half], axis=0)], axis=0)
    window = (
        (frame[None, :] >= frame[:, None]).astype(jnp.float32)
        + (frame[None, :] <= (length - 1 - frame)[:, None]).astype(jnp.float32)
    )
    numer = exact_product(window, squares) - 2.0 * corr
    counts = jnp.asarray((length - steps).astype(np.float32))
    return jnp.transpose(numer / counts[:, None])


def per_device(displacements):
    local_frames, _, atom_count = displacements.shape
    groups = lax.axis_size("frames")
    atom_total = atom_count * lax.axis_size("atoms")
    members = lax.axis_size("atoms")
    partial_sum = jnp.sum(displacements, axis=2).reshape(1, local_frames * 3)
    spread = jnp.broadcast_to(partial_sum, (members, local_frames * 3))
    gathered = lax.all_to_all(spread, "atoms", split_axis=0, concat_axis=0, tiled=True)
    count = atom_count // groups
    blocks = jnp.transpose(displacements.reshape(local_frames, 3, groups, count), (2, 0, 1, 3))
    blocks = blocks.reshape(groups, local_frames * 3 * count)
    gathered, blocks = lax.optimization_barrier((gathered, blocks))
    summed = jnp.sum(gathered, axis=0).reshape(local_frames, 3)
    drift_row = jnp.broadcast_to((summed / atom_total)[:, :, None], (local_frames, 3, count))
    outgoing = blocks - drift_row.reshape(1, local_frames * 3 * count)
    length = local_frames * groups
    *parts, outgoing = lax.optimization_barrier((*table_parts(length, length // 2), outgoing))
    moved = lax.all_to_all(outgoing, "frames", split_axis=0, concat_axis=0, tiled=True)
    series = moved.reshape(length, 3 * count)
    return lag_table(series, count, parts)


def solution(mesh):
    placed = (P("frames", None, "atoms"),)
    return jax.shard_map(
        per_device,
        mesh=mesh,
        in_specs=placed,
        out_specs=P(("atoms", "frames"), None),
        check_vma=False,
    )
```

```python
import numpy as np

import jax
import jax.numpy as jnp
from jax import lax
from jax.sharding import PartitionSpec as P


def angle_tables(length, split):
    frame = np.arange(length, dtype=np.int64)
    low = np.arange(split, dtype=np.int64)
    high = np.arange(length // split, dtype=np.int64) * split
    coarse = (high[:, None] * frame[None, :]) % (2 * length) * (np.pi / length)
    fine = (low[:, None] * frame[None, :]) % (2 * length) * (np.pi / length)
    return np.cos(coarse), np.sin(coarse), np.cos(fine), np.sin(fine)


def table_parts(length, rows):
    split = 32
    blocks = rows // split
    cos_hi, sin_hi, cos_lo, sin_lo = angle_tables(length, split)
    first = np.concatenate([cos_hi[:blocks], sin_hi[:blocks]]).astype(np.float32)
    second = np.concatenate([-sin_hi[:blocks], cos_hi[:blocks]]).astype(np.float32)
    return [jnp.asarray(t) for t in (first, second, cos_lo.astype(np.float32), sin_lo.astype(np.float32))]


def spectral_table(length, rows, parts):
    first, second, cos_lo, sin_lo = parts
    table = first[:, None, :] * cos_lo[None, :, :] + second[:, None, :] * sin_lo[None, :, :]
    table = table.reshape(2 * rows, length)
    frame = jnp.arange(length, dtype=jnp.int32)
    both_quarters = jnp.where(frame % 4 < 2, 1.0, -1.0).astype(jnp.float32)
    row = jnp.arange(2 * rows, dtype=jnp.int32)
    return jnp.where((row == rows)[:, None], both_quarters[None, :], table)


def split_three(values):
    first = lax.reduce_precision(values, exponent_bits=8, mantissa_bits=7)
    rest = values - first
    second = lax.reduce_precision(rest, exponent_bits=8, mantissa_bits=7)
    third = rest - second
    return jnp.concatenate([first, second, third], axis=1).astype(jnp.bfloat16)


def exact_product(matrix, values):
    width = values.shape[1]
    out = jnp.dot(
        matrix.astype(jnp.bfloat16), split_three(values), preferred_element_type=jnp.float32
    )
    return out[:, :width] + out[:, width : 2 * width] + out[:, 2 * width :]


def lag_table(series, count, parts):
    length = series.shape[0]
    half = length // 2
    width = 3 * count
    frame = jnp.arange(length, dtype=jnp.int32)
    lower = (frame[None, :] <= frame[:, None]).astype(jnp.float32)
    positions = exact_product(lower, series)
    squares = jnp.sum((positions * positions).reshape(length, 3, count), axis=1)
    table_full = spectral_table(length, half, parts)
    steps = np.arange(length)
    parity = jnp.asarray(np.where(steps % 2 == 0, 1.0, -1.0).astype(np.float32))
    quarter_cos = np.where(steps % 4 == 0, 1.0, np.where(steps % 4 == 2, -1.0, 0.0)).astype(np.float32)
    signed = jnp.concatenate([positions, positions * parity[:, None]], axis=1)
    spectrum = jnp.dot(table_full, signed, precision=lax.Precision.HIGHEST)
    real_part = spectrum[:half]
    imag_part = spectrum[half:] * jnp.asarray((steps[:half] != 0).astype(np.float32))[:, None]
    power = jnp.sum((real_part * real_part + imag_part * imag_part).reshape(half, 2, 3, count), axis=2)
    plus, minus = spectrum[half, :width], spectrum[half, width:]
    middle = jnp.sum((0.5 * (plus * plus + minus * minus)).reshape(3, count), axis=0) * (2.0 / (2 * length))
    weight = jnp.asarray((np.where(steps[:half] == 0, 1.0, 2.0) / (2 * length)).astype(np.float32))
    coef = (power * weight[:, None, None]).reshape(half, 2 * count)
    sign_q = parity[:half]
    coef = jnp.concatenate([coef, coef * sign_q[:, None]], axis=1)
    table = jnp.concatenate([table_full[:half, :half], jnp.asarray(quarter_cos[None, :half])], axis=0)
    folded = jnp.dot(table, coef, precision=lax.Precision.HIGHEST)
    sign_m = parity[: half + 1, None]
    quarter = jnp.asarray(quarter_cos[: half + 1, None])
    near = folded[:, :count] + sign_m * folded[:, count : 2 * count] + middle[None, :] * quarter
    far = folded[:, 2 * count : 3 * count] + sign_m * folded[:, 3 * count :] + middle[None, :] * quarter
    corr = jnp.concatenate([near, jnp.flip(far[1:half], axis=0)], axis=0)
    window = (
        (frame[None, :] >= frame[:, None]).astype(jnp.float32)
        + (frame[None, :] <= (length - 1 - frame)[:, None]).astype(jnp.float32)
    )
    parts_t = lax.dot_general(
        split_three(squares), window.astype(jnp.bfloat16), (((0,), (1,)), ((), ())),
        preferred_element_type=jnp.float32,
    )
    spans = parts_t[:count] + parts_t[count : 2 * count] + parts_t[2 * count :]
    counts = jnp.asarray((length - steps).astype(np.float32))
    return (spans - 2.0 * jnp.transpose(corr)) / counts[None, :]


def per_device(displacements):
    local_frames, _, atom_count = displacements.shape
    groups = lax.axis_size("frames")
    atom_total = atom_count * lax.axis_size("atoms")
    members = lax.axis_size("atoms")
    partial_sum = jnp.sum(displacements, axis=2).reshape(1, local_frames * 3)
    spread = jnp.broadcast_to(partial_sum, (members, local_frames * 3))
    gathered = lax.all_to_all(spread, "atoms", split_axis=0, concat_axis=0, tiled=True)
    count = atom_count // groups
    blocks = jnp.transpose(displacements.reshape(local_frames, 3, groups, count), (2, 0, 1, 3))
    blocks = blocks.reshape(groups, local_frames * 3 * count)
    gathered, blocks = lax.optimization_barrier((gathered, blocks))
    summed = jnp.sum(gathered, axis=0).reshape(local_frames, 3)
    drift_row = jnp.broadcast_to((summed / atom_total)[:, :, None], (local_frames, 3, count))
    outgoing = blocks - drift_row.reshape(1, local_frames * 3 * count)
    length = local_frames * groups
    *parts, outgoing = lax.optimization_barrier((*table_parts(length, length // 2), outgoing))
    moved = lax.all_to_all(outgoing, "frames", split_axis=0, concat_axis=0, tiled=True)
    series = moved.reshape(length, 3 * count)
    return lag_table(series, count, parts)


def solution(mesh):
    placed = (P("frames", None, "atoms"),)
    return jax.shard_map(
        per_device,
        mesh=mesh,
        in_specs=placed,
        out_specs=P(("atoms", "frames"), None),
        check_vma=False,
    )
```

```python
import numpy as np

import jax
import jax.numpy as jnp
from jax import lax
from jax.sharding import PartitionSpec as P


def angle_tables(length, split):
    frame = np.arange(length, dtype=np.int64)
    low = np.arange(split, dtype=np.int64)
    high = np.arange(length // split, dtype=np.int64) * split
    coarse = (high[:, None] * frame[None, :]) % (2 * length) * (np.pi / length)
    fine = (low[:, None] * frame[None, :]) % (2 * length) * (np.pi / length)
    return np.cos(coarse), np.sin(coarse), np.cos(fine), np.sin(fine)


def table_parts(length, rows):
    split = 32
    blocks = rows // split
    cos_hi, sin_hi, cos_lo, sin_lo = angle_tables(length, split)
    first = np.concatenate([cos_hi[:blocks], sin_hi[:blocks]]).astype(np.float32)
    second = np.concatenate([-sin_hi[:blocks], cos_hi[:blocks]]).astype(np.float32)
    return [jnp.asarray(t) for t in (first, second, cos_lo.astype(np.float32), sin_lo.astype(np.float32))]


def spectral_table(length, rows, parts):
    first, second, cos_lo, sin_lo = parts
    table = first[:, None, :] * cos_lo[None, :, :] + second[:, None, :] * sin_lo[None, :, :]
    table = table.reshape(2 * rows, length)
    frame = jnp.arange(length, dtype=jnp.int32)
    both_quarters = jnp.where(frame % 4 < 2, 1.0, -1.0).astype(jnp.float32)
    row = jnp.arange(2 * rows, dtype=jnp.int32)
    return jnp.where((row == rows)[:, None], both_quarters[None, :], table)


def split_three(values):
    first = lax.reduce_precision(values, exponent_bits=8, mantissa_bits=7)
    rest = values - first
    second = lax.reduce_precision(rest, exponent_bits=8, mantissa_bits=7)
    third = rest - second
    return jnp.concatenate([first, second, third], axis=1).astype(jnp.bfloat16)


def exact_product(matrix, values):
    width = values.shape[1]
    out = jnp.dot(
        matrix.astype(jnp.bfloat16), split_three(values), preferred_element_type=jnp.float32
    )
    return out[:, :width] + out[:, width : 2 * width] + out[:, 2 * width :]


def lag_table(series, count, parts):
    length = series.shape[0]
    half = length // 2
    width = 3 * count
    frame = jnp.arange(length, dtype=jnp.int32)
    lower = (frame[None, :] <= frame[:, None]).astype(jnp.float32)
    positions = exact_product(lower, series)
    squares = jnp.sum((positions * positions).reshape(length, 3, count), axis=1)
    table_full = spectral_table(length, half, parts)
    steps = np.arange(length)
    parity = jnp.asarray(np.where(steps % 2 == 0, 1.0, -1.0).astype(np.float32))
    quarter_cos = np.where(steps % 4 == 0, 1.0, np.where(steps % 4 == 2, -1.0, 0.0)).astype(np.float32)
    signed = jnp.concatenate([positions, positions * parity[:, None]], axis=1)
    table_one = lax.reduce_precision(table_full, exponent_bits=8, mantissa_bits=7)
    table_rest = table_full - table_one
    table_two = lax.reduce_precision(table_rest, exponent_bits=8, mantissa_bits=7)
    table_three = table_rest - table_two
    pieces = split_three(signed)
    wide = 2 * width
    by_one = jnp.dot(table_one.astype(jnp.bfloat16), pieces, preferred_element_type=jnp.float32)
    by_two = jnp.dot(table_two.astype(jnp.bfloat16), pieces[:, : 2 * wide], preferred_element_type=jnp.float32)
    by_three = jnp.dot(table_three.astype(jnp.bfloat16), pieces[:, :wide], preferred_element_type=jnp.float32)
    spectrum = (
        (by_one[:, 2 * wide :] + by_two[:, wide:] + by_three)
        + (by_one[:, wide : 2 * wide] + by_two[:, :wide])
        + by_one[:, :wide]
    )
    real_part = spectrum[:half]
    imag_part = spectrum[half:] * jnp.asarray((steps[:half] != 0).astype(np.float32))[:, None]
    power = jnp.sum((real_part * real_part + imag_part * imag_part).reshape(half, 2, 3, count), axis=2)
    plus, minus = spectrum[half, :width], spectrum[half, width:]
    middle = jnp.sum((0.5 * (plus * plus + minus * minus)).reshape(3, count), axis=0) * (2.0 / (2 * length))
    weight = jnp.asarray((np.where(steps[:half] == 0, 1.0, 2.0) / (2 * length)).astype(np.float32))
    coef = (power * weight[:, None, None]).reshape(half, 2 * count)
    sign_q = parity[:half]
    coef = jnp.concatenate([coef, coef * sign_q[:, None]], axis=1)
    table = jnp.concatenate([table_full[:half, :half], jnp.asarray(quarter_cos[None, :half])], axis=0)
    folded = jnp.dot(table, coef, precision=lax.Precision.HIGHEST)
    sign_m = parity[: half + 1, None]
    quarter = jnp.asarray(quarter_cos[: half + 1, None])
    near = folded[:, :count] + sign_m * folded[:, count : 2 * count] + middle[None, :] * quarter
    far = folded[:, 2 * count : 3 * count] + sign_m * folded[:, 3 * count :] + middle[None, :] * quarter
    corr = jnp.concatenate([near, jnp.flip(far[1:half], axis=0)], axis=0)
    window = (
        (frame[None, :] >= frame[:, None]).astype(jnp.float32)
        + (frame[None, :] <= (length - 1 - frame)[:, None]).astype(jnp.float32)
    )
    parts_t = lax.dot_general(
        split_three(squares), window.astype(jnp.bfloat16), (((0,), (1,)), ((), ())),
        preferred_element_type=jnp.float32,
    )
    spans = parts_t[:count] + parts_t[count : 2 * count] + parts_t[2 * count :]
    counts = jnp.asarray((length - steps).astype(np.float32))
    return (spans - 2.0 * jnp.transpose(corr)) / counts[None, :]


def per_device(displacements):
    local_frames, _, atom_count = displacements.shape
    groups = lax.axis_size("frames")
    atom_total = atom_count * lax.axis_size("atoms")
    members = lax.axis_size("atoms")
    partial_sum = jnp.sum(displacements, axis=2).reshape(1, local_frames * 3)
    spread = jnp.broadcast_to(partial_sum, (members, local_frames * 3))
    gathered = lax.all_to_all(spread, "atoms", split_axis=0, concat_axis=0, tiled=True)
    count = atom_count // groups
    blocks = jnp.transpose(displacements.reshape(local_frames, 3, groups, count), (2, 0, 1, 3))
    blocks = blocks.reshape(groups, local_frames * 3 * count)
    gathered, blocks = lax.optimization_barrier((gathered, blocks))
    summed = jnp.sum(gathered, axis=0).reshape(local_frames, 3)
    drift_row = jnp.broadcast_to((summed / atom_total)[:, :, None], (local_frames, 3, count))
    outgoing = blocks - drift_row.reshape(1, local_frames * 3 * count)
    length = local_frames * groups
    *parts, outgoing = lax.optimization_barrier((*table_parts(length, length // 2), outgoing))
    moved = lax.all_to_all(outgoing, "frames", split_axis=0, concat_axis=0, tiled=True)
    series = moved.reshape(length, 3 * count)
    return lag_table(series, count, parts)


def solution(mesh):
    placed = (P("frames", None, "atoms"),)
    return jax.shard_map(
        per_device,
        mesh=mesh,
        in_specs=placed,
        out_specs=P(("atoms", "frames"), None),
        check_vma=False,
    )
```

```python
import numpy as np

import jax
import jax.numpy as jnp
from jax import lax
from jax.sharding import PartitionSpec as P


def angle_tables(length, split):
    frame = np.arange(length, dtype=np.int64)
    low = np.arange(split, dtype=np.int64)
    high = np.arange(length // split, dtype=np.int64) * split
    coarse = (high[:, None] * frame[None, :]) % (2 * length) * (np.pi / length)
    fine = (low[:, None] * frame[None, :]) % (2 * length) * (np.pi / length)
    return np.cos(coarse), np.sin(coarse), np.cos(fine), np.sin(fine)


def table_parts(length, rows):
    split = 32
    blocks = rows // split
    cos_hi, sin_hi, cos_lo, sin_lo = angle_tables(length, split)
    first = np.concatenate([cos_hi[:blocks], sin_hi[:blocks]]).astype(np.float32)
    second = np.concatenate([-sin_hi[:blocks], cos_hi[:blocks]]).astype(np.float32)
    return [jnp.asarray(t) for t in (first, second, cos_lo.astype(np.float32), sin_lo.astype(np.float32))]


def spectral_table(length, rows, parts):
    first, second, cos_lo, sin_lo = parts
    table = first[:, None, :] * cos_lo[None, :, :] + second[:, None, :] * sin_lo[None, :, :]
    table = table.reshape(2 * rows, length)
    frame = jnp.arange(length, dtype=jnp.int32)
    both_quarters = jnp.where(frame % 4 < 2, 1.0, -1.0).astype(jnp.float32)
    row = jnp.arange(2 * rows, dtype=jnp.int32)
    return jnp.where((row == rows)[:, None], both_quarters[None, :], table)


def split_three(values):
    first = lax.reduce_precision(values, exponent_bits=8, mantissa_bits=7)
    rest = values - first
    second = lax.reduce_precision(rest, exponent_bits=8, mantissa_bits=7)
    third = rest - second
    return jnp.concatenate([first, second, third], axis=1).astype(jnp.bfloat16)


def exact_product(matrix, values):
    width = values.shape[1]
    out = jnp.dot(
        matrix.astype(jnp.bfloat16), split_three(values), preferred_element_type=jnp.float32
    )
    return out[:, :width] + out[:, width : 2 * width] + out[:, 2 * width :]


def lag_table(series, count, parts, lower, window):
    length = series.shape[0]
    half = length // 2
    width = 3 * count
    frame = jnp.arange(length, dtype=jnp.int32)
    positions = exact_product(lower, series)
    squares = jnp.sum((positions * positions).reshape(length, 3, count), axis=1)
    table_full = spectral_table(length, half, parts)
    steps = np.arange(length)
    parity = jnp.asarray(np.where(steps % 2 == 0, 1.0, -1.0).astype(np.float32))
    quarter_cos = np.where(steps % 4 == 0, 1.0, np.where(steps % 4 == 2, -1.0, 0.0)).astype(np.float32)
    signed = jnp.concatenate([positions, positions * parity[:, None]], axis=1)
    spectrum = jnp.dot(table_full, signed, precision=lax.Precision.HIGHEST)
    real_part = spectrum[:half]
    imag_part = spectrum[half:] * jnp.asarray((steps[:half] != 0).astype(np.float32))[:, None]
    power = jnp.sum((real_part * real_part + imag_part * imag_part).reshape(half, 2, 3, count), axis=2)
    plus, minus = spectrum[half, :width], spectrum[half, width:]
    middle = jnp.sum((0.5 * (plus * plus + minus * minus)).reshape(3, count), axis=0) * (2.0 / (2 * length))
    weight = jnp.asarray((np.where(steps[:half] == 0, 1.0, 2.0) / (2 * length)).astype(np.float32))
    coef = (power * weight[:, None, None]).reshape(half, 2 * count)
    sign_q = parity[:half]
    coef = jnp.concatenate([coef, coef * sign_q[:, None]], axis=1)
    table = jnp.concatenate([table_full[:half, :half], jnp.asarray(quarter_cos[None, :half])], axis=0)
    folded = jnp.dot(table, coef, precision=lax.Precision.HIGHEST)
    sign_m = parity[: half + 1, None]
    quarter = jnp.asarray(quarter_cos[: half + 1, None])
    near = folded[:, :count] + sign_m * folded[:, count : 2 * count] + middle[None, :] * quarter
    far = folded[:, 2 * count : 3 * count] + sign_m * folded[:, 3 * count :] + middle[None, :] * quarter
    corr = jnp.concatenate([near, jnp.flip(far[1:half], axis=0)], axis=0)
    parts_t = lax.dot_general(
        split_three(squares), window, (((0,), (1,)), ((), ())),
        preferred_element_type=jnp.float32,
    )
    spans = parts_t[:count] + parts_t[count : 2 * count] + parts_t[2 * count :]
    counts = jnp.asarray((length - steps).astype(np.float32))
    return (spans - 2.0 * jnp.transpose(corr)) / counts[None, :]


def per_device(displacements):
    local_frames, _, atom_count = displacements.shape
    groups = lax.axis_size("frames")
    atom_total = atom_count * lax.axis_size("atoms")
    members = lax.axis_size("atoms")
    partial_sum = jnp.sum(displacements, axis=2).reshape(1, local_frames * 3)
    spread = jnp.broadcast_to(partial_sum, (members, local_frames * 3))
    gathered = lax.all_to_all(spread, "atoms", split_axis=0, concat_axis=0, tiled=True)
    count = atom_count // groups
    blocks = jnp.transpose(displacements.reshape(local_frames, 3, groups, count), (2, 0, 1, 3))
    blocks = blocks.reshape(groups, local_frames * 3 * count)
    gathered, blocks = lax.optimization_barrier((gathered, blocks))
    summed = jnp.sum(gathered, axis=0).reshape(local_frames, 3)
    drift_row = jnp.broadcast_to((summed / atom_total)[:, :, None], (local_frames, 3, count))
    outgoing = blocks - drift_row.reshape(1, local_frames * 3 * count)
    length = local_frames * groups
    frame = jnp.arange(length, dtype=jnp.int32)
    lower = (frame[None, :] <= frame[:, None]).astype(jnp.bfloat16)
    window = (
        (frame[None, :] >= frame[:, None]).astype(jnp.float32)
        + (frame[None, :] <= (length - 1 - frame)[:, None]).astype(jnp.float32)
    ).astype(jnp.bfloat16)
    *parts, lower, window, outgoing = lax.optimization_barrier(
        (*table_parts(length, length // 2), lower, window, outgoing)
    )
    moved = lax.all_to_all(outgoing, "frames", split_axis=0, concat_axis=0, tiled=True)
    series = moved.reshape(length, 3 * count)
    return lag_table(series, count, parts, lower, window)


def solution(mesh):
    placed = (P("frames", None, "atoms"),)
    return jax.shard_map(
        per_device,
        mesh=mesh,
        in_specs=placed,
        out_specs=P(("atoms", "frames"), None),
        check_vma=False,
    )
```
